32 devices in a mesh: tm: 2 (over x), gx: 4 (over y, core), gy: 4 (over z).
Axes of the slice: x: 2, y: 2, z: 4, core: 2. Of those that a mesh axis runs over, the one named last changes fastest.
Arguments:
- potential: float32 [64, 4, 128, 512], P('tm', None, 'gx', 'gy'), may hold values from -6 to 6
- source: float32 [64, 4, 128, 512], P('tm', None, 'gx', 'gy'), may hold values from -6 to 6
- region: int32 [128, 512], P('gx', 'gy'), may hold values from 0 to 7
- level_index: int32 [64], P('tm'), may hold values from 0 to 15
- reluctivity: float32 [16, 8], replicated, may hold values from 0.2 to 1
- saturation: float32 [8], replicated, may hold values from 0.05 to 0.4
- inverse: float32 [64, 128, 32], P('tm', 'gx'), may hold values from -1 to 1
- transmit: float32 [64, 4], P('tm', 'gx'), may hold values from 0.05 to 1.1
Outputs:
- correction: float32 [64, 4, 128, 512], P('tm', None, 'gx', 'gy')
The draws below stay inside these ranges and needn't reach their ends.
All inputs are finite; a program needn't handle non-finite values.
Results may differ from the reference program's by a relative error of at most 0.00012.
Values sent between devices are 32-bit elements; how exact they have to be, the bound alone decides.
No kernel may reach another device: no remote copies, remote signals or barrier semaphores. Data moves between devices by JAX's collectives and lax.ppermute only.
A program may use at most 64 MiB of HBM per device.

```python
import math
import jax
import jax.numpy as jnp
from jax import lax

PERIOD_SAMPLES = 64
P_SIZE = 4
CX = 32
KINDS = 8
LEVELS = 16
NX = 128
NY = 512
LINE_BLOCKS = 4


def draw_inverse(key, part):
    key_diag, key_off, key_corner = jax.random.split(key, 3)
    row_ids = lax.iota(jnp.int32, NX) % CX
    col_ids = lax.iota(jnp.int32, CX)
    diagonal = jax.random.uniform(key_diag, (PERIOD_SAMPLES, NX, CX), jnp.float32, 0.6, 1.0)
    off_diag = jax.random.truncated_normal(key_off, -3.0, 3.0, (PERIOD_SAMPLES, NX, CX), jnp.float32) * (0.35 / math.sqrt(CX))
    corner = jax.random.uniform(key_corner, (PERIOD_SAMPLES, NX, CX), jnp.float32, 0.85, 0.95)
    on_diag = (row_ids[:, None] == col_ids[None, :])[None]
    on_corner = ((row_ids[:, None] == CX - 1) & (col_ids[None, :] == 0))[None]
    return jnp.where(on_diag, diagonal, jnp.where(on_corner, corner, off_diag))


def draw_transmit(key, part):
    category_key, gradual_key, quick_key, spike_key, dissipation_key = jax.random.split(key, 5)
    slow_share = 0.5
    slow_rows = jax.random.bernoulli(category_key, slow_share, (PERIOD_SAMPLES, 1))
    gradual_rate = jax.random.uniform(gradual_key, (PERIOD_SAMPLES, LINE_BLOCKS), jnp.float32, 1.0, 1.1)
    spike_mask = jax.random.bernoulli(spike_key, min(2.0 / LINE_BLOCKS, 0.5), (PERIOD_SAMPLES, LINE_BLOCKS))
    dissipation_factor = jax.random.uniform(dissipation_key, (PERIOD_SAMPLES, LINE_BLOCKS), jnp.float32, 0.5, 0.8)
    gradual_rate = jnp.where(spike_mask, gradual_rate * dissipation_factor, gradual_rate)
    fast_rate = jax.random.uniform(quick_key, (PERIOD_SAMPLES, LINE_BLOCKS), jnp.float32, 0.05, 0.2)
    return jnp.where(slow_rows, gradual_rate, fast_rate)


def set_ends(drawn, key, low, largest):
    longest = drawn.shape.index(max(drawn.shape))
    spots = []
    for shift in (0, 1):
        where = [jax.random.randint(jax.random.fold_in(key, axis), (), 0, length) for axis, length in enumerate(drawn.shape)]
        where[longest] = (where[longest] + shift) % drawn.shape[longest]
        spots.append(tuple(where))
    return drawn.at[spots[0]].set(low).at[spots[1]].set(largest)


def levels(rng, dims, shards, smallest, top_value):
    gain = 1.0
    for axis_at, parts in shards:
        draws = jax.random.uniform(jax.random.fold_in(jax.random.fold_in(rng, 6), axis_at), (parts,), jnp.float32, smallest / len(shards), top_value / len(shards))
        gain = gain * jnp.repeat(jnp.exp(draws), dims[axis_at] // parts).reshape((-1,) + (1,) * (len(dims) - 1 - axis_at))
    return gain


def bell_draw(own_key, extent, spread, limit, pieces=(), dtype=jnp.bfloat16):
    result = spread * jax.random.normal(own_key, extent, jnp.float32)
    if pieces:
        result = result * levels(own_key, extent, pieces, -0.22, 0.18)
    return jnp.clip(result, -limit, limit).astype(dtype)


def setup_inputs(seed: int = 0) -> dict:
    arg_keys = jax.random.split(jax.random.key(seed), 9)
    potential = bell_draw(arg_keys[0], (PERIOD_SAMPLES, P_SIZE, NX, NY), 1.0, 6.0, ((0, 2), (2, 4), (3, 4)), jnp.float32)
    source = bell_draw(arg_keys[1], (PERIOD_SAMPLES, P_SIZE, NX, NY), 1.0, 6.0, ((0, 2), (2, 4), (3, 4)), jnp.float32)
    region = set_ends(jax.random.randint(arg_keys[2], (NX, NY), 0, KINDS), jax.random.fold_in(arg_keys[2], 1), 0, KINDS - 1).astype(jnp.int32)
    level_index = set_ends(jax.random.randint(arg_keys[3], (PERIOD_SAMPLES,), 0, LEVELS), jax.random.fold_in(arg_keys[3], 1), 0, LEVELS - 1).astype(jnp.int32)
    reluctivity = jnp.clip(jnp.exp(jax.random.uniform(arg_keys[4], (LEVELS, KINDS), jnp.float32, math.log(0.2), math.log(1.0))), 0.2, 1.0)
    saturation = jnp.clip(jnp.exp(jax.random.uniform(arg_keys[5], (KINDS,), jnp.float32, math.log(0.05), math.log(0.4))), 0.05, 0.4)
    inverse = draw_inverse(jax.random.fold_in(arg_keys[8], 71), 0)
    transmit = draw_transmit(jax.random.fold_in(arg_keys[8], 71), 0)
    return dict(potential=potential, source=source, region=region, level_index=level_index, reluctivity=reluctivity, saturation=saturation, inverse=inverse, transmit=transmit)


axial_coupling = 0.5

def fourier_rows(first_row, row_count, sample_ids, sample_count):
    row_ids = first_row + lax.iota(jnp.int32, row_count)
    half_count = sample_count // 2
    harmonic = jnp.where(row_ids <= half_count, row_ids, row_ids - half_count)
    phase_index = harmonic[:, None] * sample_ids[None, :] % sample_count
    angle_value = phase_index.astype(jnp.float32) * (2.0 * math.pi / sample_count)
    dft_table = jnp.where((row_ids <= half_count)[:, None], jnp.cos(angle_value), jnp.sin(angle_value))
    return dft_table * math.sqrt(2.0 / sample_count)

def reference(potential, source, region, level_index, reluctivity, saturation, inverse, transmit):
    sample_count = potential.shape[0]
    planes = potential.shape[1]
    cells_x = inverse.shape[2]
    blocks = inverse.shape[1] // cells_x
    width_x = potential.shape[2]
    width_y = potential.shape[3]
    padded_kind = jnp.pad(region, 1)[:-1, :-1]
    slope_cell = saturation[padded_kind]
    base_rows = reluctivity[level_index]

    def one_sample(sample_items):
        field_now, load_now, base_row = sample_items
        padded = jnp.pad(field_now, ((0, 0), (1, 1), (1, 1)))
        corner = padded[:, :-1, :-1]
        step_x = padded[:, 1:, :-1] - corner
        step_y = padded[:, :-1, 1:] - corner
        base_cell = base_row[padded_kind]
        reluct = base_cell[None] * (1.0 + slope_cell * (step_x * step_x + step_y * step_y))
        flux_x = reluct * step_x
        flux_y = reluct * step_y
        curl_part = flux_x[:, :-1, 1:] - flux_x[:, 1:, 1:] + flux_y[:, 1:, :-1] - flux_y[:, 1:, 1:]
        zero_plane = jnp.zeros_like(field_now[:1])
        plane_below = jnp.concatenate([zero_plane, field_now[:-1]], axis=0)
        plane_above = jnp.concatenate([field_now[1:], zero_plane], axis=0)
        return curl_part + axial_coupling * (2.0 * field_now - plane_below - plane_above) - load_now
    residual_time = lax.map(one_sample, (potential, source, base_rows))
    dft_table = fourier_rows(0, sample_count, lax.iota(jnp.int32, sample_count), sample_count)
    spectra = jnp.einsum('qs,spij->qpij', dft_table, residual_time, precision=lax.Precision.HIGHEST)
    blocks_inv = inverse.reshape(sample_count, blocks, cells_x, cells_x)
    shaped = spectra.reshape(sample_count, planes, blocks, cells_x, width_y)
    solved = jnp.einsum('qkab,qpkbj->qpkaj', blocks_inv, shaped, precision=lax.Precision.HIGHEST)
    line_tail = solved[:, :, :, cells_x - 1, :]
    factor = transmit * blocks_inv[:, :, cells_x - 1, 0]

    def advance(carried, scan_items):
        tail_k, factor_k = scan_items
        return (tail_k + factor_k[:, None, None] * carried, carried)
    chain_end, incoming = lax.scan(advance, jnp.zeros((sample_count, planes, width_y), jnp.float32), (jnp.moveaxis(line_tail, 2, 0), factor.T))
    incoming = jnp.moveaxis(incoming, 0, 2)
    injected = transmit[:, None, :, None] * incoming
    correction = solved + injected[:, :, :, None, :] * blocks_inv[:, :, :, 0][:, None, :, :, None]
    return correction.reshape(sample_count, planes, width_x, width_y)
```

```python
import math

import jax
import jax.numpy as jnp
from jax import lax
from jax.sharding import PartitionSpec as P

axial_coupling = 0.5


def shifted(block, axes, sizes, delta):
    coords = [(i, j) for i in range(sizes[0]) for j in range(sizes[1])]
    route = []
    for i, j in coords:
        si, sj = i - delta[0], j - delta[1]
        if 0 <= si < sizes[0] and 0 <= sj < sizes[1]:
            route.append((si * sizes[1] + sj, i * sizes[1] + j))
    return lax.ppermute(block, axes, route)


def fourier_rows(row_ids, sample_ids, sample_count):
    half_count = sample_count // 2
    harmonic = jnp.where(row_ids <= half_count, row_ids, row_ids - half_count)
    phase_index = harmonic[:, None] * sample_ids[None, :] % sample_count
    angle_value = phase_index.astype(jnp.float32) * (2.0 * math.pi / sample_count)
    dft_table = jnp.where(
        (row_ids <= half_count)[:, None], jnp.cos(angle_value), jnp.sin(angle_value)
    )
    return dft_table * math.sqrt(2.0 / sample_count)


def local(potential, source, region, level_index, reluctivity, saturation, inverse, transmit):
    samples_dev, planes, cells_x, cells_y = potential.shape
    n_tm = lax.axis_size("tm")
    n_gx = lax.axis_size("gx")
    n_gy = lax.axis_size("gy")
    me_tm = lax.axis_index("tm")
    me_gx = lax.axis_index("gx")
    sample_count = samples_dev * n_tm
    grid = ("gx", "gy")
    sizes = (n_gx, n_gy)
    a = potential
    regf = region.astype(jnp.float32)

    msg_xlo = jnp.concatenate(
        [a[:, :, cells_x - 1, :].reshape(samples_dev * planes, cells_y), regf[cells_x - 1][None]], axis=0
    )
    msg_ylo = jnp.concatenate(
        [a[:, :, :, cells_y - 1].reshape(samples_dev * planes, cells_x), regf[:, cells_y - 1][None]], axis=0
    )
    got_xlo = shifted(msg_xlo, grid, sizes, (1, 0))
    got_ylo = shifted(msg_ylo, grid, sizes, (0, 1))
    got_xhi = shifted(a[:, :, 0, :], grid, sizes, (-1, 0))
    got_yhi = shifted(a[:, :, :, 0], grid, sizes, (0, -1))
    got_c1 = shifted(a[:, :, cells_x - 1, 0], grid, sizes, (1, -1))
    got_c2 = shifted(a[:, :, 0, cells_y - 1], grid, sizes, (-1, 1))

    xlo = got_xlo[:-1].reshape(samples_dev, planes, cells_y)
    reg_xlo = got_xlo[-1]
    ylo = got_ylo[:-1].reshape(samples_dev, planes, cells_x)
    reg_ylo = got_ylo[-1]
    xhi, yhi = got_xhi, got_yhi

    onehot = (level_index[:, None] == lax.iota(jnp.int32, reluctivity.shape[0])[None, :]).astype(jnp.float32)
    base_rows = jnp.sum(onehot[:, :, None] * reluctivity[None], axis=1)

    reg_xm = jnp.concatenate([reg_xlo[None, :].astype(jnp.int32), region[:-1]], axis=0)
    reg_ym = jnp.concatenate([reg_ylo[:, None].astype(jnp.int32), region[:, :-1]], axis=1)

    def reluct_of(kind, s_rows):
        out = s_rows[:, 0][:, None, None, None] + jnp.zeros(kind.shape, jnp.float32)[None, None]
        for k in range(1, s_rows.shape[-1]):
            out = jnp.where((kind == k)[None, None], s_rows[:, k][:, None, None, None], out)
        sl = jnp.full(kind.shape, saturation[0], jnp.float32)
        for k in range(1, saturation.shape[0]):
            sl = jnp.where(kind == k, saturation[k], sl)
        return out, sl[None, None]

    a_xp = jnp.concatenate([a[:, :, 1:, :], xhi[:, :, None, :]], axis=2)
    a_yp = jnp.concatenate([a[:, :, :, 1:], yhi[:, :, :, None]], axis=3)
    a_xm = jnp.concatenate([xlo[:, :, None, :], a[:, :, :-1, :]], axis=2)
    a_ym = jnp.concatenate([ylo[:, :, :, None], a[:, :, :, :-1]], axis=3)
    top = jnp.concatenate([xlo[:, :, 1:], got_c1[:, :, None]], axis=2)
    inner = jnp.concatenate([a[:, :, :-1, 1:], yhi[:, :, :-1, None]], axis=3)
    a_xm_yp = jnp.concatenate([top[:, :, None, :], inner], axis=2)
    bottom = jnp.concatenate([got_c2[:, :, None], xhi[:, :, :-1]], axis=2)
    inner2 = jnp.concatenate([ylo[:, :, 1:, None], a[:, :, 1:, :-1]], axis=3)
    a_xp_ym = jnp.concatenate([inner2, bottom[:, :, None, :]], axis=2)

    b0, s0 = reluct_of(region, base_rows)
    b1, s1 = reluct_of(reg_xm, base_rows)
    b2, s2 = reluct_of(reg_ym, base_rows)

    sx0 = a_xp - a
    sy0 = a_yp - a
    r0 = b0 * (1.0 + s0 * (sx0 * sx0 + sy0 * sy0))
    fx0 = r0 * sx0
    fy0 = r0 * sy0
    sx1 = a - a_xm
    sy1 = a_xm_yp - a_xm
    fx1 = b1 * (1.0 + s1 * (sx1 * sx1 + sy1 * sy1)) * sx1
    sx2 = a_xp_ym - a_ym
    sy2 = a - a_ym
    fy2 = b2 * (1.0 + s2 * (sx2 * sx2 + sy2 * sy2)) * sy2
    curl_part = fx1 - fx0 + fy2 - fy0
    zero_plane = jnp.zeros_like(a[:, :1])
    plane_below = jnp.concatenate([zero_plane, a[:, :-1]], axis=1)
    plane_above = jnp.concatenate([a[:, 1:], zero_plane], axis=1)
    residual_time = curl_part + axial_coupling * (2.0 * a - plane_below - plane_above) - source

    sample_ids = me_tm * samples_dev + lax.iota(jnp.int32, samples_dev)
    q_dev = samples_dev

    spectra_planes = []
    pending = []
    for p in range(planes):
        flat = residual_time[:, p].reshape(samples_dev, cells_x * cells_y)
        own_tab = fourier_rows(me_tm * q_dev + lax.iota(jnp.int32, q_dev), sample_ids, sample_count)
        acc = jnp.dot(own_tab, flat, precision=lax.Precision.HIGHEST, preferred_element_type=jnp.float32)
        for d in range(1, n_tm):
            owner = (me_tm + d) % n_tm
            tab = fourier_rows(owner * q_dev + lax.iota(jnp.int32, q_dev), sample_ids, sample_count)
            part = jnp.dot(tab, flat, precision=lax.Precision.HIGHEST, preferred_element_type=jnp.float32)
            route = [(i, (i + d) % n_tm) for i in range(n_tm)]
            acc = acc + lax.ppermute(part, "tm", route)
        spectra_planes.append(acc.reshape(q_dev, cells_x, cells_y))
    spectra = jnp.stack(spectra_planes, axis=1)

    solved = jnp.einsum("qab,qpbj->qpaj", inverse, spectra, precision=lax.Precision.HIGHEST)
    line_tail = solved[:, :, cells_x - 1, :]
    gain_here = transmit[:, 0] * inverse[:, cells_x - 1, 0]

    tails = []
    gains = []
    for d in range(n_gx - 1, 0, -1):
        route = [(i, i + d) for i in range(n_gx - d)]
        tails.append(lax.ppermute(line_tail, "gx", route))
        gains.append(lax.ppermute(gain_here, "gx", route))
    carried = jnp.zeros_like(line_tail)
    for idx, d in enumerate(range(n_gx - 1, 0, -1)):
        stepped = tails[idx] + gains[idx][:, None, None] * carried
        carried = jnp.where(me_gx >= d, stepped, carried)
    injected = transmit[:, 0][:, None, None] * carried
    correction = solved + injected[:, :, None, :] * inverse[:, :, 0][:, None, :, None]
    return correction


def solution(mesh):
    in_specs = (
        P("tm", None, "gx", "gy"),
        P("tm", None, "gx", "gy"),
        P("gx", "gy"),
        P("tm"),
        P(),
        P(),
        P("tm", "gx", None),
        P("tm", "gx"),
    )
    out_specs = P("tm", None, "gx", "gy")
    return jax.shard_map(local, mesh=mesh, in_specs=in_specs, out_specs=out_specs, check_vma=False)
```

```python
import functools
import math

import jax
import jax.numpy as jnp
from jax import lax
from jax.experimental import pallas as pl
from jax.experimental.pallas import tpu as pltpu
from jax.sharding import PartitionSpec as P

axial_coupling = 0.5
SAMPLE_BLOCK = 8


def shifted(block, axes, sizes, delta):
    route = []
    for i in range(sizes[0]):
        for j in range(sizes[1]):
            si, sj = i - delta[0], j - delta[1]
            if 0 <= si < sizes[0] and 0 <= sj < sizes[1]:
                route.append((si * sizes[1] + sj, i * sizes[1] + j))
    return lax.ppermute(block, axes, route)


def fourier_rows(row_ids, sample_ids, sample_count):
    half_count = sample_count // 2
    harmonic = jnp.where(row_ids <= half_count, row_ids, row_ids - half_count)
    phase_index = harmonic[:, None] * sample_ids[None, :] % sample_count
    angle_value = phase_index.astype(jnp.float32) * (2.0 * math.pi / sample_count)
    dft_table = jnp.where(
        (row_ids <= half_count)[:, None], jnp.cos(angle_value), jnp.sin(angle_value)
    )
    return dft_table * math.sqrt(2.0 / sample_count)


def residual_kernel(has_lo, has_hi, kinds, *refs):
    it = iter(refs)
    a_ref = next(it)
    lo_ref = next(it) if has_lo else None
    hi_ref = next(it) if has_hi else None
    src_ref, xlo_ref, xhi_ref, ylo_ref, yhi_ref, c1_ref, c2_ref, base_ref = [next(it) for _ in range(8)]
    reg_ref, reg_xlo_ref, reg_ylo_ref, sat_ref, sat_xlo_ref, sat_ylo_ref, out_ref = [next(it) for _ in range(7)]
    blk = pl.program_id(0)
    n_s, nx, ny = a_ref.shape
    ix = lax.broadcasted_iota(jnp.int32, (nx, ny), 0)
    iy = lax.broadcasted_iota(jnp.int32, (nx, ny), 1)
    ix_col = lax.broadcasted_iota(jnp.int32, (nx, 1), 0)
    iy_row = lax.broadcasted_iota(jnp.int32, (1, ny), 1)
    reg = reg_ref[...]
    reg_xlo = reg_xlo_ref[...]
    reg_ylo = reg_ylo_ref[...]
    sat = sat_ref[...]
    sat_xlo = sat_xlo_ref[...]
    sat_ylo = sat_ylo_ref[...]

    def lookup(kind, s_glob):
        out = jnp.full(kind.shape, base_ref[s_glob, 0], jnp.float32)
        for k in range(1, kinds):
            out = jnp.where(kind == k, base_ref[s_glob, k], out)
        return out

    def body(s, carry):
        s_glob = blk * n_s + s
        a = a_ref[s]
        row_hi = xhi_ref[pl.ds(s, 1), :]
        row_lo = xlo_ref[pl.ds(s, 1), :]
        col_hi = yhi_ref[s]
        col_lo = ylo_ref[s]
        c1 = c1_ref[0, s_glob]
        c2 = c2_ref[0, s_glob]
        base = lookup(reg, s_glob)
        base_xlo = lookup(reg_xlo, s_glob)
        base_ylo = lookup(reg_ylo, s_glob)
        a_xp = jnp.where(ix == nx - 1, row_hi, pltpu.roll(a, nx - 1, 0))
        a_yp = jnp.where(iy == ny - 1, col_hi, pltpu.roll(a, ny - 1, 1))
        sx = a_xp - a
        sy = a_yp - a
        rel = base * (1.0 + sat * (sx * sx + sy * sy))
        fx = rel * sx
        fy = rel * sy
        lo_yp = jnp.where(iy_row == ny - 1, c1, pltpu.roll(row_lo, ny - 1, 1))
        sx_l = a[0:1, :] - row_lo
        sy_l = lo_yp - row_lo
        fx_l = base_xlo * (1.0 + sat_xlo * (sx_l * sx_l + sy_l * sy_l)) * sx_l
        lo_xp = jnp.where(ix_col == nx - 1, c2, pltpu.roll(col_lo, nx - 1, 0))
        sx_c = lo_xp - col_lo
        sy_c = a[:, 0:1] - col_lo
        fy_c = base_ylo * (1.0 + sat_ylo * (sx_c * sx_c + sy_c * sy_c)) * sy_c
        fx_down = jnp.where(ix == 0, fx_l, pltpu.roll(fx, 1, 0))
        fy_left = jnp.where(iy == 0, fy_c, pltpu.roll(fy, 1, 1))
        curl = fx_down - fx + fy_left - fy
        axial = 2.0 * a
        if has_lo:
            axial = axial - lo_ref[s]
        if has_hi:
            axial = axial - hi_ref[s]
        out_ref[s] = curl + axial_coupling * axial - src_ref[s]
        return carry

    lax.fori_loop(0, n_s, body, 0)


def residual_plane(p, a, src, xlo, xhi, ylo_c, yhi_c, c1, c2, base_rows, reg, reg_xlo, reg_ylo, sat, sat_xlo, sat_ylo):
    n_s, planes, nx, ny = a.shape
    kinds = base_rows.shape[1]
    sb = min(SAMPLE_BLOCK, n_s)
    has_lo = p > 0
    has_hi = p < planes - 1
    tile = lambda q: pl.BlockSpec((sb, None, nx, ny), lambda i: (i, q, 0, 0))
    vmem_whole = pl.BlockSpec(memory_space=pltpu.VMEM)
    smem_whole = pl.BlockSpec(memory_space=pltpu.SMEM)
    in_specs = [tile(p)]
    args = [a]
    if has_lo:
        in_specs.append(tile(p - 1))
        args.append(a)
    if has_hi:
        in_specs.append(tile(p + 1))
        args.append(a)
    in_specs += [
        tile(p),
        pl.BlockSpec((None, sb, ny), lambda i: (p, i, 0)),
        pl.BlockSpec((None, sb, ny), lambda i: (p, i, 0)),
        pl.BlockSpec((None, sb, nx, 1), lambda i: (p, i, 0, 0)),
        pl.BlockSpec((None, sb, nx, 1), lambda i: (p, i, 0, 0)),
        smem_whole,
        smem_whole,
        smem_whole,
    ] + [vmem_whole] * 6
    args += [src, xlo, xhi, ylo_c, yhi_c, c1[p:p + 1], c2[p:p + 1], base_rows, reg, reg_xlo, reg_ylo, sat, sat_xlo, sat_ylo]
    return pl.pallas_call(
        functools.partial(residual_kernel, has_lo, has_hi, kinds),
        grid=(n_s // sb,),
        in_specs=in_specs,
        out_specs=pl.BlockSpec((sb, nx, ny), lambda i: (i, 0, 0)),
        out_shape=jax.ShapeDtypeStruct((n_s, nx, ny), jnp.float32),
        name="residual_plane",
    )(*args)


def local(potential, source, region, level_index, reluctivity, saturation, inverse, transmit):
    samples_dev, planes, cells_x, cells_y = potential.shape
    n_tm = lax.axis_size("tm")
    n_gx = lax.axis_size("gx")
    n_gy = lax.axis_size("gy")
    me_tm = lax.axis_index("tm")
    me_gx = lax.axis_index("gx")
    sample_count = samples_dev * n_tm
    grid = ("gx", "gy")
    sizes = (n_gx, n_gy)
    a = potential
    regf = region.astype(jnp.float32)
    kinds = reluctivity.shape[1]

    msg_xlo = jnp.concatenate(
        [a[:, :, cells_x - 1, :].reshape(samples_dev * planes, cells_y), regf[cells_x - 1][None]], axis=0
    )
    msg_ylo = jnp.concatenate(
        [a[:, :, :, cells_y - 1].reshape(samples_dev * planes, cells_x), regf[:, cells_y - 1][None]], axis=0
    )
    got_xlo = shifted(msg_xlo, grid, sizes, (1, 0))
    got_ylo = shifted(msg_ylo, grid, sizes, (0, 1))
    xhi = shifted(a[:, :, 0, :], grid, sizes, (-1, 0))
    yhi = shifted(a[:, :, :, 0], grid, sizes, (0, -1))
    c1 = shifted(a[:, :, cells_x - 1, 0], grid, sizes, (1, -1))
    c2 = shifted(a[:, :, 0, cells_y - 1], grid, sizes, (-1, 1))

    xlo = got_xlo[:-1].reshape(samples_dev, planes, cells_y)
    reg_xlo = got_xlo[-1].astype(jnp.int32)[None, :]
    ylo = got_ylo[:-1].reshape(samples_dev, planes, cells_x)
    reg_ylo = got_ylo[-1].astype(jnp.int32)[:, None]
    xlo = jnp.transpose(xlo, (1, 0, 2))
    xhi = jnp.transpose(xhi, (1, 0, 2))
    ylo_c = jnp.transpose(ylo, (1, 0, 2))[..., None]
    yhi_c = jnp.transpose(yhi, (1, 0, 2))[..., None]
    c1 = c1.T
    c2 = c2.T

    onehot = (level_index[:, None] == lax.iota(jnp.int32, reluctivity.shape[0])[None, :]).astype(jnp.float32)
    base_rows = jnp.sum(onehot[:, :, None] * reluctivity[None], axis=1)

    def sat_of(kind):
        out = jnp.full(kind.shape, saturation[0], jnp.float32)
        for k in range(1, kinds):
            out = jnp.where(kind == k, saturation[k], out)
        return out

    sat = sat_of(region)
    sat_xlo = sat_of(reg_xlo)
    sat_ylo = sat_of(reg_ylo)

    sample_ids = me_tm * samples_dev + lax.iota(jnp.int32, samples_dev)
    q_dev = samples_dev

    spectra_planes = []
    for p in range(planes):
        resid = residual_plane(
            p, a, source, xlo, xhi, ylo_c, yhi_c, c1, c2, base_rows,
            region, reg_xlo, reg_ylo, sat, sat_xlo, sat_ylo,
        )
        flat = resid.reshape(samples_dev, cells_x * cells_y)
        parts = []
        for d in range(1, n_tm):
            owner = (me_tm + d) % n_tm
            tab = fourier_rows(owner * q_dev + lax.iota(jnp.int32, q_dev), sample_ids, sample_count)
            part = jnp.dot(tab, flat, precision=lax.Precision.HIGHEST, preferred_element_type=jnp.float32)
            route = [(i, (i + d) % n_tm) for i in range(n_tm)]
            parts.append(lax.ppermute(part, "tm", route))
        own_tab = fourier_rows(me_tm * q_dev + lax.iota(jnp.int32, q_dev), sample_ids, sample_count)
        acc = jnp.dot(own_tab, flat, precision=lax.Precision.HIGHEST, preferred_element_type=jnp.float32)
        for got in parts:
            acc = acc + got
        spectra_planes.append(acc.reshape(q_dev, cells_x, cells_y))
    spectra = jnp.stack(spectra_planes, axis=1)

    solved = jnp.einsum("qab,qpbj->qpaj", inverse, spectra, precision=lax.Precision.HIGHEST)
    line_tail = solved[:, :, cells_x - 1, :]
    gain_here = transmit[:, 0] * inverse[:, cells_x - 1, 0]

    tails = []
    gains = []
    for d in range(n_gx - 1, 0, -1):
        route = [(i, i + d) for i in range(n_gx - d)]
        tails.append(lax.ppermute(line_tail, "gx", route))
        gains.append(lax.ppermute(gain_here, "gx", route))
    carried = jnp.zeros_like(line_tail)
    for idx, d in enumerate(range(n_gx - 1, 0, -1)):
        stepped = tails[idx] + gains[idx][:, None, None] * carried
        carried = jnp.where(me_gx >= d, stepped, carried)
    injected = transmit[:, 0][:, None, None] * carried
    correction = solved + injected[:, :, None, :] * inverse[:, :, 0][:, None, :, None]
    return correction


def solution(mesh):
    in_specs = (
        P("tm", None, "gx", "gy"),
        P("tm", None, "gx", "gy"),
        P("gx", "gy"),
        P("tm"),
        P(),
        P(),
        P("tm", "gx", None),
        P("tm", "gx"),
    )
    out_specs = P("tm", None, "gx", "gy")
    return jax.shard_map(local, mesh=mesh, in_specs=in_specs, out_specs=out_specs, check_vma=False)
```

```python
import functools
import math

import jax
import jax.numpy as jnp
from jax import lax
from jax.experimental import pallas as pl
from jax.experimental.pallas import tpu as pltpu
from jax.sharding import PartitionSpec as P

axial_coupling = 0.5
SAMPLE_BLOCK = 8


def shifted(block, axes, sizes, delta):
    route = []
    for i in range(sizes[0]):
        for j in range(sizes[1]):
            si, sj = i - delta[0], j - delta[1]
            if 0 <= si < sizes[0] and 0 <= sj < sizes[1]:
                route.append((si * sizes[1] + sj, i * sizes[1] + j))
    return lax.ppermute(block, axes, route)


def fourier_rows(row_ids, sample_ids, sample_count):
    half_count = sample_count // 2
    harmonic = jnp.where(row_ids <= half_count, row_ids, row_ids - half_count)
    phase_index = harmonic[:, None] * sample_ids[None, :] % sample_count
    angle_value = phase_index.astype(jnp.float32) * (2.0 * math.pi / sample_count)
    dft_table = jnp.where(
        (row_ids <= half_count)[:, None], jnp.cos(angle_value), jnp.sin(angle_value)
    )
    return dft_table * math.sqrt(2.0 / sample_count)


def row_to_col(row, ix, iy):
    full = jnp.broadcast_to(row, ix.shape)
    return jnp.sum(jnp.where(ix == iy, full, 0.0), axis=1, keepdims=True)


def col_to_row(col, ix, iy):
    full = jnp.broadcast_to(col, ix.shape)
    return jnp.sum(jnp.where(ix == iy, full, 0.0), axis=0, keepdims=True)


def edges_kernel(a_ref, x31_ref, x0_ref, y127_ref, y0_ref):
    n_s, planes, nx, ny = a_ref.shape
    ix = lax.broadcasted_iota(jnp.int32, (nx, ny), 0)
    iy = lax.broadcasted_iota(jnp.int32, (nx, ny), 1)

    def body(s, carry):
        for p in range(planes):
            a = a_ref[s, p]
            x31_ref[p, pl.ds(s, 1), :] = a[nx - 1:nx, :]
            x0_ref[p, pl.ds(s, 1), :] = a[0:1, :]
            y127_ref[p, pl.ds(s, 1), :] = col_to_row(a[:, ny - 1:ny], ix, iy)
            y0_ref[p, pl.ds(s, 1), :] = col_to_row(a[:, 0:1], ix, iy)
        return carry

    lax.fori_loop(0, n_s, body, 0)


def edges(a):
    n_s, planes, nx, ny = a.shape
    sb = min(SAMPLE_BLOCK, n_s)
    out = jax.ShapeDtypeStruct((planes, n_s, ny), jnp.float32)
    spec = pl.BlockSpec((planes, sb, ny), lambda i: (0, i, 0))
    return pl.pallas_call(
        edges_kernel,
        grid=(n_s // sb,),
        in_specs=[pl.BlockSpec((sb, planes, nx, ny), lambda i: (i, 0, 0, 0))],
        out_specs=[spec] * 4,
        out_shape=[out] * 4,
        name="halo_edges",
    )(a)


def residual_kernel(kinds, a_ref, src_ref, xlo_ref, xhi_ref, ylo_ref, yhi_ref, c1_ref, c2_ref, base_ref, sat_ref,
                    reg_ref, reg_xlo_ref, reg_ylo_ref, out_ref):
    blk = pl.program_id(0)
    n_s, planes, nx, ny = a_ref.shape
    ix = lax.broadcasted_iota(jnp.int32, (nx, ny), 0)
    iy = lax.broadcasted_iota(jnp.int32, (nx, ny), 1)
    ix_col = lax.broadcasted_iota(jnp.int32, (nx, 1), 0)
    iy_row = lax.broadcasted_iota(jnp.int32, (1, ny), 1)
    reg = reg_ref[...]
    reg_xlo = reg_xlo_ref[...]
    reg_ylo = row_to_col(reg_ylo_ref[...].astype(jnp.float32), ix, iy).astype(jnp.int32)

    def lookup(kind, table, row):
        out = jnp.full(kind.shape, table[row, 0] if row is not None else table[0], jnp.float32)
        for k in range(1, kinds):
            out = jnp.where(kind == k, table[row, k] if row is not None else table[k], out)
        return out

    sat = lookup(reg, sat_ref, None)
    sat_xlo = lookup(reg_xlo, sat_ref, None)
    sat_ylo = lookup(reg_ylo, sat_ref, None)

    def body(s, carry):
        s_glob = blk * n_s + s
        base = lookup(reg, base_ref, s_glob)
        base_xlo = lookup(reg_xlo, base_ref, s_glob)
        base_ylo = lookup(reg_ylo, base_ref, s_glob)
        tiles = [a_ref[s, p] for p in range(planes)]
        for p in range(planes):
            a = tiles[p]
            row_hi = xhi_ref[p, pl.ds(s, 1), :]
            row_lo = xlo_ref[p, pl.ds(s, 1), :]
            col_hi = row_to_col(yhi_ref[p, pl.ds(s, 1), :], ix, iy)
            col_lo = row_to_col(ylo_ref[p, pl.ds(s, 1), :], ix, iy)
            c1 = c1_ref[p, s_glob]
            c2 = c2_ref[p, s_glob]
            a_xp = jnp.where(ix == nx - 1, row_hi, pltpu.roll(a, nx - 1, 0))
            a_yp = jnp.where(iy == ny - 1, col_hi, pltpu.roll(a, ny - 1, 1))
            sx = a_xp - a
            sy = a_yp - a
            rel = base * (1.0 + sat * (sx * sx + sy * sy))
            fx = rel * sx
            fy = rel * sy
            lo_yp = jnp.where(iy_row == ny - 1, c1, pltpu.roll(row_lo, ny - 1, 1))
            sx_l = a[0:1, :] - row_lo
            sy_l = lo_yp - row_lo
            fx_l = base_xlo * (1.0 + sat_xlo * (sx_l * sx_l + sy_l * sy_l)) * sx_l
            lo_xp = jnp.where(ix_col == nx - 1, c2, pltpu.roll(col_lo, nx - 1, 0))
            sx_c = lo_xp - col_lo
            sy_c = a[:, 0:1] - col_lo
            fy_c = base_ylo * (1.0 + sat_ylo * (sx_c * sx_c + sy_c * sy_c)) * sy_c
            fx_down = jnp.where(ix == 0, fx_l, pltpu.roll(fx, 1, 0))
            fy_left = jnp.where(iy == 0, fy_c, pltpu.roll(fy, 1, 1))
            curl = fx_down - fx + fy_left - fy
            axial = 2.0 * a
            if p > 0:
                axial = axial - tiles[p - 1]
            if p < planes - 1:
                axial = axial - tiles[p + 1]
            out_ref[p, s] = curl + axial_coupling * axial - src_ref[s, p]
        return carry

    lax.fori_loop(0, n_s, body, 0)


def residual(a, src, xlo, xhi, ylo, yhi, c1, c2, base_rows, saturation, reg, reg_xlo, reg_ylo):
    n_s, planes, nx, ny = a.shape
    kinds = base_rows.shape[1]
    sb = min(SAMPLE_BLOCK, n_s)
    tile = pl.BlockSpec((sb, planes, nx, ny), lambda i: (i, 0, 0, 0))
    edge = pl.BlockSpec((planes, sb, ny), lambda i: (0, i, 0))
    vmem_whole = pl.BlockSpec(memory_space=pltpu.VMEM)
    smem_whole = pl.BlockSpec(memory_space=pltpu.SMEM)
    return pl.pallas_call(
        functools.partial(residual_kernel, kinds),
        grid=(n_s // sb,),
        in_specs=[tile, tile, edge, edge, edge, edge] + [smem_whole] * 4 + [vmem_whole] * 3,
        out_specs=pl.BlockSpec((planes, sb, nx, ny), lambda i: (0, i, 0, 0)),
        out_shape=jax.ShapeDtypeStruct((planes, n_s, nx, ny), jnp.float32),
        name="residual",
    )(a, src, xlo, xhi, ylo, yhi, c1, c2, base_rows, saturation, reg, reg_xlo, reg_ylo)


def local(potential, source, region, level_index, reluctivity, saturation, inverse, transmit):
    samples_dev, planes, cells_x, cells_y = potential.shape
    n_tm = lax.axis_size("tm")
    n_gx = lax.axis_size("gx")
    n_gy = lax.axis_size("gy")
    me_tm = lax.axis_index("tm")
    me_gx = lax.axis_index("gx")
    sample_count = samples_dev * n_tm
    grid = ("gx", "gy")
    sizes = (n_gx, n_gy)
    rows = planes * samples_dev

    e_x31, e_x0, e_y127, e_y0 = edges(potential)
    regf = region.astype(jnp.float32)
    pad = jnp.zeros((7, cells_y), jnp.float32)
    reg_col = jnp.pad(regf[:, cells_y - 1], (0, cells_y - cells_x))
    msg_xlo = jnp.concatenate([e_x31.reshape(rows, cells_y), regf[cells_x - 1][None], pad], axis=0)
    msg_ylo = jnp.concatenate([e_y127.reshape(rows, cells_y), reg_col[None], pad], axis=0)
    got_xlo = shifted(msg_xlo, grid, sizes, (1, 0))
    got_ylo = shifted(msg_ylo, grid, sizes, (0, 1))
    xhi = shifted(e_x0, grid, sizes, (-1, 0))
    yhi = shifted(e_y0, grid, sizes, (0, -1))
    c1 = shifted(e_x31[:, :, 0], grid, sizes, (1, -1))
    c2 = shifted(e_x0[:, :, cells_y - 1], grid, sizes, (-1, 1))

    xlo = got_xlo[:rows].reshape(planes, samples_dev, cells_y)
    reg_xlo = got_xlo[rows:rows + 1].astype(jnp.int32)
    ylo = got_ylo[:rows].reshape(planes, samples_dev, cells_y)
    reg_ylo = got_ylo[rows:rows + 1].astype(jnp.int32)

    onehot = (level_index[:, None] == lax.iota(jnp.int32, reluctivity.shape[0])[None, :]).astype(jnp.float32)
    base_rows = jnp.sum(onehot[:, :, None] * reluctivity[None], axis=1)

    resid = residual(potential, source, xlo, xhi, ylo, yhi, c1, c2, base_rows, saturation,
                     region, reg_xlo, reg_ylo)

    sample_ids = me_tm * samples_dev + lax.iota(jnp.int32, samples_dev)
    q_dev = samples_dev

    spectra_planes = []
    for p in range(planes):
        plane = resid[p]
        parts = []
        for d in range(1, n_tm):
            owner = (me_tm + d) % n_tm
            tab = fourier_rows(owner * q_dev + lax.iota(jnp.int32, q_dev), sample_ids, sample_count)
            part = jnp.einsum("qs,sxy->qxy", tab, plane, precision=lax.Precision.HIGHEST)
            route = [(i, (i + d) % n_tm) for i in range(n_tm)]
            parts.append(lax.ppermute(part, "tm", route))
        own_tab = fourier_rows(me_tm * q_dev + lax.iota(jnp.int32, q_dev), sample_ids, sample_count)
        acc = jnp.einsum("qs,sxy->qxy", own_tab, plane, precision=lax.Precision.HIGHEST)
        for got in parts:
            acc = acc + got
        spectra_planes.append(acc)
    spectra = jnp.stack(spectra_planes, axis=1)

    solved = jnp.einsum("qab,qpbj->qpaj", inverse, spectra, precision=lax.Precision.HIGHEST)
    line_tail = solved[:, :, cells_x - 1, :]
    gain_here = transmit[:, 0] * inverse[:, cells_x - 1, 0]
    msg_tail = jnp.concatenate([line_tail, jnp.broadcast_to(gain_here[:, None, None], (q_dev, 1, cells_y))], axis=1)

    carried = jnp.zeros_like(line_tail)
    for d in range(n_gx - 1, 0, -1):
        route = [(i, i + d) for i in range(n_gx - d)]
        got = lax.ppermute(msg_tail, "gx", route)
        stepped = got[:, :planes] + got[:, planes:planes + 1] * carried
        carried = jnp.where(me_gx >= d, stepped, carried)
    injected = transmit[:, 0][:, None, None] * carried
    correction = solved + injected[:, :, None, :] * inverse[:, :, 0][:, None, :, None]
    return correction


def solution(mesh):
    in_specs = (
        P("tm", None, "gx", "gy"),
        P("tm", None, "gx", "gy"),
        P("gx", "gy"),
        P("tm"),
        P(),
        P(),
        P("tm", "gx", None),
        P("tm", "gx"),
    )
    out_specs = P("tm", None, "gx", "gy")
    return jax.shard_map(local, mesh=mesh, in_specs=in_specs, out_specs=out_specs, check_vma=False)
```

```python
import functools
import math

import jax
import jax.numpy as jnp
from jax import lax
from jax.experimental import pallas as pl
from jax.experimental.pallas import tpu as pltpu
from jax.sharding import PartitionSpec as P

axial_coupling = 0.5
SAMPLE_BLOCK = 8


def shifted(block, axes, sizes, delta):
    route = []
    for i in range(sizes[0]):
        for j in range(sizes[1]):
            si, sj = i - delta[0], j - delta[1]
            if 0 <= si < sizes[0] and 0 <= sj < sizes[1]:
                route.append((si * sizes[1] + sj, i * sizes[1] + j))
    return lax.ppermute(block, axes, route)


def fourier_rows(row_ids, sample_ids, sample_count):
    half_count = sample_count // 2
    harmonic = jnp.where(row_ids <= half_count, row_ids, row_ids - half_count)
    phase_index = harmonic[:, None] * sample_ids[None, :] % sample_count
    angle_value = phase_index.astype(jnp.float32) * (2.0 * math.pi / sample_count)
    dft_table = jnp.where(
        (row_ids <= half_count)[:, None], jnp.cos(angle_value), jnp.sin(angle_value)
    )
    return dft_table * math.sqrt(2.0 / sample_count)


def edges_kernel(a_ref, x31_ref, x0_ref, c127_ref, c0_ref):
    n_s, planes, nx, ny = a_ref.shape
    iy = lax.broadcasted_iota(jnp.int32, (nx, ny), 1)

    def body(s, carry):
        acc127, acc0 = carry
        for p in range(planes):
            t = s * planes + p
            a = a_ref[s, p]
            x31_ref[p, pl.ds(s, 1), :] = a[nx - 1:nx, :]
            x0_ref[p, pl.ds(s, 1), :] = a[0:1, :]
            acc127 = jnp.where(iy == t, pltpu.roll(a, lax.rem(t + 1, ny), 1), acc127)
            acc0 = jnp.where(iy == t, pltpu.roll(a, t, 1), acc0)
        return acc127, acc0

    zero = jnp.zeros((nx, ny), jnp.float32)
    acc127, acc0 = lax.fori_loop(0, n_s, body, (zero, zero))
    c127_ref[...] = acc127
    c0_ref[...] = acc0


def edges(a):
    n_s, planes, nx, ny = a.shape
    vmem = pl.BlockSpec(memory_space=pltpu.VMEM)
    row = jax.ShapeDtypeStruct((planes, n_s, ny), jnp.float32)
    col = jax.ShapeDtypeStruct((nx, ny), jnp.float32)
    return pl.pallas_call(
        edges_kernel,
        in_specs=[vmem],
        out_specs=[vmem] * 4,
        out_shape=[row, row, col, col],
        name="halo_edges",
    )(a)


def residual_kernel(kinds, a_ref, src_ref, xlo_ref, xhi_ref, ylo_ref, yhi_ref, own0_ref, c2_ref, bt_ref,
                    c1_ref, base_ref, sat_ref, reg_ref, reg_xlo_ref, reg_ycol_ref, out_ref):
    blk = pl.program_id(0)
    n_s, planes, nx, ny = a_ref.shape
    ix = lax.broadcasted_iota(jnp.int32, (nx, ny), 0)
    iy = lax.broadcasted_iota(jnp.int32, (nx, ny), 1)
    iy_row = lax.broadcasted_iota(jnp.int32, (1, ny), 1)
    reg = reg_ref[...]
    reg_xlo = reg_xlo_ref[...]
    reg_ycol = reg_ycol_ref[...]

    def lookup(kind, pick):
        out = jnp.broadcast_to(pick(0), kind.shape).astype(jnp.float32)
        for k in range(1, kinds):
            out = jnp.where(kind == k, pick(k), out)
        return out

    sat = lookup(reg, lambda k: sat_ref[k])
    sat_xlo = lookup(reg_xlo, lambda k: sat_ref[k])
    c_lo = ylo_ref[...]
    lo_xp = jnp.where(ix == nx - 1, c2_ref[...], pltpu.roll(c_lo, nx - 1, 0))
    sx_c = lo_xp - c_lo
    sy_c = own0_ref[...] - c_lo
    kind_c = jnp.broadcast_to(reg_ycol, (nx, ny))
    base_c = lookup(kind_c, lambda k: bt_ref[k:k + 1, :])
    sat_c = lookup(kind_c, lambda k: sat_ref[k])
    fy_cols = base_c * (1.0 + sat_c * (sx_c * sx_c + sy_c * sy_c)) * sy_c
    c_hi = yhi_ref[...]

    def body(s, carry):
        s_glob = blk * n_s + s
        base = lookup(reg, lambda k: base_ref[s_glob, k])
        base_xlo = lookup(reg_xlo, lambda k: base_ref[s_glob, k])
        tiles = [a_ref[s, p] for p in range(planes)]
        for p in range(planes):
            t = s_glob * planes + p
            a = tiles[p]
            row_hi = xhi_ref[p, pl.ds(s, 1), :]
            row_lo = xlo_ref[p, pl.ds(s, 1), :]
            c1 = c1_ref[0, t]
            col_hi = pltpu.roll(c_hi, lax.rem(ny - 1 - t + ny, ny), 1)
            a_xp = jnp.where(ix == nx - 1, row_hi, pltpu.roll(a, nx - 1, 0))
            a_yp = jnp.where(iy == ny - 1, col_hi, pltpu.roll(a, ny - 1, 1))
            sx = a_xp - a
            sy = a_yp - a
            rel = base * (1.0 + sat * (sx * sx + sy * sy))
            fx = rel * sx
            fy = rel * sy
            lo_yp = jnp.where(iy_row == ny - 1, c1, pltpu.roll(row_lo, ny - 1, 1))
            sx_l = a[0:1, :] - row_lo
            sy_l = lo_yp - row_lo
            fx_l = base_xlo * (1.0 + sat_xlo * (sx_l * sx_l + sy_l * sy_l)) * sx_l
            fy_c = pltpu.roll(fy_cols, lax.rem(ny - t, ny), 1)
            fx_down = jnp.where(ix == 0, fx_l, pltpu.roll(fx, 1, 0))
            fy_left = jnp.where(iy == 0, fy_c, pltpu.roll(fy, 1, 1))
            curl = fx_down - fx + fy_left - fy
            axial = 2.0 * a
            if p > 0:
                axial = axial - tiles[p - 1]
            if p < planes - 1:
                axial = axial - tiles[p + 1]
            out_ref[p, s] = curl + axial_coupling * axial - src_ref[s, p]
        return carry

    lax.fori_loop(0, n_s, body, 0)


def residual(a, src, xlo, xhi, ylo, yhi, own0, c2, bt, c1, base_rows, saturation, reg, reg_xlo, reg_ycol):
    n_s, planes, nx, ny = a.shape
    kinds = base_rows.shape[1]
    sb = min(SAMPLE_BLOCK, n_s)
    tile = pl.BlockSpec((sb, planes, nx, ny), lambda i: (i, 0, 0, 0))
    edge = pl.BlockSpec((planes, sb, ny), lambda i: (0, i, 0))
    vmem_whole = pl.BlockSpec(memory_space=pltpu.VMEM)
    smem_whole = pl.BlockSpec(memory_space=pltpu.SMEM)
    return pl.pallas_call(
        functools.partial(residual_kernel, kinds),
        grid=(n_s // sb,),
        in_specs=[tile, tile, edge, edge] + [vmem_whole] * 5 + [smem_whole] * 3 + [vmem_whole] * 3,
        out_specs=pl.BlockSpec((planes, sb, nx, ny), lambda i: (0, i, 0, 0)),
        out_shape=jax.ShapeDtypeStruct((planes, n_s, nx, ny), jnp.float32),
        name="residual",
    )(a, src, xlo, xhi, ylo, yhi, own0, c2, bt, c1, base_rows, saturation, reg, reg_xlo, reg_ycol)


def local(potential, source, region, level_index, reluctivity, saturation, inverse, transmit):
    samples_dev, planes, cells_x, cells_y = potential.shape
    n_tm = lax.axis_size("tm")
    n_gx = lax.axis_size("gx")
    n_gy = lax.axis_size("gy")
    me_tm = lax.axis_index("tm")
    me_gx = lax.axis_index("gx")
    sample_count = samples_dev * n_tm
    q_dev = samples_dev
    grid = ("gx", "gy")
    sizes = (n_gx, n_gy)
    rows = planes * samples_dev

    gain_here = transmit[:, 0] * inverse[:, cells_x - 1, 0]
    own_info = jnp.concatenate([inverse[:, cells_x - 1, :], gain_here[:, None]], axis=1)
    infos = [own_info]
    for d in range(1, n_tm):
        infos.append(lax.ppermute(own_info, "tm", [(i, (i - d) % n_tm) for i in range(n_tm)]))
    info_all = jnp.concatenate(infos, axis=0)
    gain_all = info_all[:, cells_x]
    gains_prev = []
    for d in range(n_gx - 1, 0, -1):
        gains_prev.append(lax.ppermute(gain_all, "gx", [(i, i + d) for i in range(n_gx - d)]))

    e_x31, e_x0, e_c127, e_c0 = edges(potential)
    regf = region.astype(jnp.float32)
    pad = jnp.zeros((7, cells_y), jnp.float32)
    msg_xlo = jnp.concatenate([e_x31.reshape(rows, cells_y), regf[cells_x - 1][None], pad], axis=0)
    got_xlo = shifted(msg_xlo, grid, sizes, (1, 0))
    xhi = shifted(e_x0, grid, sizes, (-1, 0))
    ylo = shifted(e_c127, grid, sizes, (0, 1))
    yhi = shifted(e_c0, grid, sizes, (0, -1))
    reg_ycol = shifted(region[:, cells_y - 1:cells_y], grid, sizes, (0, 1))
    c1 = shifted(e_c0[cells_x - 1:cells_x], grid, sizes, (1, -1))
    c2 = shifted(e_c127[0:1], grid, sizes, (-1, 1))

    xlo = got_xlo[:rows].reshape(planes, samples_dev, cells_y)
    reg_xlo = got_xlo[rows:rows + 1].astype(jnp.int32)

    onehot = (level_index[:, None] == lax.iota(jnp.int32, reluctivity.shape[0])[None, :]).astype(jnp.float32)
    base_rows = jnp.sum(onehot[:, :, None] * reluctivity[None], axis=1)
    tile_sample = jnp.minimum(lax.iota(jnp.int32, cells_y) // planes, samples_dev - 1)
    bt = base_rows[tile_sample].T

    resid = residual(potential, source, xlo, xhi, ylo, yhi, e_c0, c2, bt, c1, base_rows, saturation,
                     region, reg_xlo, reg_ycol)

    sample_ids = me_tm * samples_dev + lax.iota(jnp.int32, samples_dev)
    tabs = [
        fourier_rows(((me_tm + d) % n_tm) * q_dev + lax.iota(jnp.int32, q_dev), sample_ids, sample_count)
        for d in range(n_tm)
    ]
    row_last = info_all[:, :cells_x].reshape(n_tm, q_dev, cells_x)
    out_planes = []
    for p in range(planes):
        plane = resid[p]
        parts = [jnp.einsum("qs,sxy->qxy", tabs[d], plane, precision=lax.Precision.HIGHEST) for d in range(n_tm)]
        got_parts = [
            lax.ppermute(parts[d], "tm", [(i, (i + d) % n_tm) for i in range(n_tm)]) for d in range(1, n_tm)
        ]
        tails = jnp.concatenate(
            [jnp.einsum("qb,qby->qy", row_last[d], parts[d], precision=lax.Precision.HIGHEST) for d in range(n_tm)],
            axis=0,
        )
        carried = jnp.zeros_like(tails)
        for idx, d in enumerate(range(n_gx - 1, 0, -1)):
            got = lax.ppermute(tails, "gx", [(i, i + d) for i in range(n_gx - d)])
            stepped = got + gains_prev[idx][:, None] * carried
            carried = jnp.where(me_gx >= d, stepped, carried)
        carried = carried.reshape(n_tm, q_dev, cells_y)
        got_carried = [
            lax.ppermute(carried[d], "tm", [(i, (i + d) % n_tm) for i in range(n_tm)]) for d in range(1, n_tm)
        ]
        spectrum = parts[0]
        for got in got_parts:
            spectrum = spectrum + got
        carried_own = carried[0]
        for got in got_carried:
            carried_own = carried_own + got
        solved = jnp.einsum("qab,qby->qay", inverse, spectrum, precision=lax.Precision.HIGHEST)
        injected = transmit[:, 0][:, None] * carried_own
        out_planes.append(solved + injected[:, None, :] * inverse[:, :, 0][:, :, None])
    return jnp.stack(out_planes, axis=1)


def solution(mesh):
    in_specs = (
        P("tm", None, "gx", "gy"),
        P("tm", None, "gx", "gy"),
        P("gx", "gy"),
        P("tm"),
        P(),
        P(),
        P("tm", "gx", None),
        P("tm", "gx"),
    )
    out_specs = P("tm", None, "gx", "gy")
    return jax.shard_map(local, mesh=mesh, in_specs=in_specs, out_specs=out_specs, check_vma=False)
```

```python
import functools
import math

import jax
import jax.numpy as jnp
from jax import lax
from jax.experimental import pallas as pl
from jax.experimental.pallas import tpu as pltpu
from jax.sharding import PartitionSpec as P

axial_coupling = 0.5
SAMPLE_BLOCK = 8


def shifted(block, axes, sizes, delta):
    route = []
    for i in range(sizes[0]):
        for j in range(sizes[1]):
            si, sj = i - delta[0], j - delta[1]
            if 0 <= si < sizes[0] and 0 <= sj < sizes[1]:
                route.append((si * sizes[1] + sj, i * sizes[1] + j))
    return lax.ppermute(block, axes, route)


def fourier_rows(row_ids, sample_ids, sample_count):
    half_count = sample_count // 2
    harmonic = jnp.where(row_ids <= half_count, row_ids, row_ids - half_count)
    phase_index = harmonic[:, None] * sample_ids[None, :] % sample_count
    angle_value = phase_index.astype(jnp.float32) * (2.0 * math.pi / sample_count)
    dft_table = jnp.where(
        (row_ids <= half_count)[:, None], jnp.cos(angle_value), jnp.sin(angle_value)
    )
    return dft_table * math.sqrt(2.0 / sample_count)


def edges_kernel(a_ref, x31_ref, x0_ref, c127_ref, c0_ref):
    n_s, planes, nx, ny = a_ref.shape
    iy = lax.broadcasted_iota(jnp.int32, (nx, ny), 1)

    def body(s, carry):
        acc127, acc0 = carry
        for p in range(planes):
            t = s * planes + p
            a = a_ref[s, p]
            x31_ref[p, pl.ds(s, 1), :] = a[nx - 1:nx, :]
            x0_ref[p, pl.ds(s, 1), :] = a[0:1, :]
            acc127 = jnp.where(iy == t, pltpu.roll(a, lax.rem(t + 1, ny), 1), acc127)
            acc0 = jnp.where(iy == t, pltpu.roll(a, t, 1), acc0)
        return acc127, acc0

    zero = jnp.zeros((nx, ny), jnp.float32)
    acc127, acc0 = lax.fori_loop(0, n_s, body, (zero, zero))
    c127_ref[...] = acc127
    c0_ref[...] = acc0


def edges(a):
    n_s, planes, nx, ny = a.shape
    vmem = pl.BlockSpec(memory_space=pltpu.VMEM)
    row = jax.ShapeDtypeStruct((planes, n_s, ny), jnp.float32)
    col = jax.ShapeDtypeStruct((nx, ny), jnp.float32)
    return pl.pallas_call(
        edges_kernel,
        in_specs=[vmem],
        out_specs=[vmem] * 4,
        out_shape=[row, row, col, col],
        name="halo_edges",
    )(a)


def residual_kernel(kinds, a_ref, src_ref, xlo_ref, xhi_ref, ylo_ref, yhi_ref, own0_ref, c2_ref, bt_ref,
                    c1_ref, base_ref, sat_ref, reg_ref, reg_xlo_ref, reg_ycol_ref, out_ref):
    blk = pl.program_id(0)
    n_s, planes, nx, ny = a_ref.shape
    ix = lax.broadcasted_iota(jnp.int32, (nx, ny), 0)
    iy = lax.broadcasted_iota(jnp.int32, (nx, ny), 1)
    iy_row = lax.broadcasted_iota(jnp.int32, (1, ny), 1)
    reg = reg_ref[...]
    reg_xlo = reg_xlo_ref[...]
    reg_ycol = reg_ycol_ref[...]

    def lookup(kind, pick):
        out = jnp.broadcast_to(pick(0), kind.shape).astype(jnp.float32)
        for k in range(1, kinds):
            out = jnp.where(kind == k, pick(k), out)
        return out

    sat = lookup(reg, lambda k: sat_ref[k])
    sat_xlo = lookup(reg_xlo, lambda k: sat_ref[k])
    c_lo = ylo_ref[...]
    lo_xp = jnp.where(ix == nx - 1, c2_ref[...], pltpu.roll(c_lo, nx - 1, 0))
    sx_c = lo_xp - c_lo
    sy_c = own0_ref[...] - c_lo
    kind_c = jnp.broadcast_to(reg_ycol, (nx, ny))
    base_c = lookup(kind_c, lambda k: bt_ref[k:k + 1, :])
    sat_c = lookup(kind_c, lambda k: sat_ref[k])
    fy_cols = base_c * (1.0 + sat_c * (sx_c * sx_c + sy_c * sy_c)) * sy_c
    c_hi = yhi_ref[...]

    def body(s, carry):
        s_glob = blk * n_s + s
        base = lookup(reg, lambda k: base_ref[s_glob, k])
        base_xlo = lookup(reg_xlo, lambda k: base_ref[s_glob, k])
        tiles = [a_ref[s, p] for p in range(planes)]
        for p in range(planes):
            t = s_glob * planes + p
            a = tiles[p]
            row_hi = xhi_ref[p, pl.ds(s, 1), :]
            row_lo = xlo_ref[p, pl.ds(s, 1), :]
            c1 = c1_ref[0, t]
            col_hi = pltpu.roll(c_hi, lax.rem(ny - 1 - t + ny, ny), 1)
            a_xp = jnp.where(ix == nx - 1, row_hi, pltpu.roll(a, nx - 1, 0))
            a_yp = jnp.where(iy == ny - 1, col_hi, pltpu.roll(a, ny - 1, 1))
            sx = a_xp - a
            sy = a_yp - a
            rel = base * (1.0 + sat * (sx * sx + sy * sy))
            fx = rel * sx
            fy = rel * sy
            lo_yp = jnp.where(iy_row == ny - 1, c1, pltpu.roll(row_lo, ny - 1, 1))
            sx_l = a[0:1, :] - row_lo
            sy_l = lo_yp - row_lo
            fx_l = base_xlo * (1.0 + sat_xlo * (sx_l * sx_l + sy_l * sy_l)) * sx_l
            fy_c = pltpu.roll(fy_cols, lax.rem(ny - t, ny), 1)
            fx_down = jnp.where(ix == 0, fx_l, pltpu.roll(fx, 1, 0))
            fy_left = jnp.where(iy == 0, fy_c, pltpu.roll(fy, 1, 1))
            curl = fx_down - fx + fy_left - fy
            axial = 2.0 * a
            if p > 0:
                axial = axial - tiles[p - 1]
            if p < planes - 1:
                axial = axial - tiles[p + 1]
            out_ref[p, s] = curl + axial_coupling * axial - src_ref[s, p]
        return carry

    lax.fori_loop(0, n_s, body, 0)


def residual(a, src, xlo, xhi, ylo, yhi, own0, c2, bt, c1, base_rows, saturation, reg, reg_xlo, reg_ycol):
    n_s, planes, nx, ny = a.shape
    kinds = base_rows.shape[1]
    sb = min(SAMPLE_BLOCK, n_s)
    tile = pl.BlockSpec((sb, planes, nx, ny), lambda i: (i, 0, 0, 0))
    edge = pl.BlockSpec((planes, sb, ny), lambda i: (0, i, 0))
    vmem_whole = pl.BlockSpec(memory_space=pltpu.VMEM)
    smem_whole = pl.BlockSpec(memory_space=pltpu.SMEM)
    return pl.pallas_call(
        functools.partial(residual_kernel, kinds),
        grid=(n_s // sb,),
        in_specs=[tile, tile, edge, edge] + [vmem_whole] * 5 + [smem_whole] * 3 + [vmem_whole] * 3,
        out_specs=pl.BlockSpec((planes, sb, nx, ny), lambda i: (0, i, 0, 0)),
        out_shape=jax.ShapeDtypeStruct((planes, n_s, nx, ny), jnp.float32),
        name="residual",
    )(a, src, xlo, xhi, ylo, yhi, own0, c2, bt, c1, base_rows, saturation, reg, reg_xlo, reg_ycol)


def local(potential, source, region, level_index, reluctivity, saturation, inverse, transmit):
    samples_dev, planes, cells_x, cells_y = potential.shape
    n_tm = lax.axis_size("tm")
    n_gx = lax.axis_size("gx")
    n_gy = lax.axis_size("gy")
    me_tm = lax.axis_index("tm")
    me_gx = lax.axis_index("gx")
    sample_count = samples_dev * n_tm
    q_dev = samples_dev
    grid = ("gx", "gy")
    sizes = (n_gx, n_gy)
    rows = planes * samples_dev

    gain_here = transmit[:, 0] * inverse[:, cells_x - 1, 0]
    own_info = jnp.concatenate([inverse[:, cells_x - 1, :], gain_here[:, None]], axis=1)
    infos = [own_info]
    for d in range(1, n_tm):
        infos.append(lax.ppermute(own_info, "tm", [(i, (i - d) % n_tm) for i in range(n_tm)]))
    info_all = jnp.concatenate(infos, axis=0)
    gain_all = info_all[:, cells_x]

    e_x31, e_x0, e_c127, e_c0 = edges(potential)
    regf = region.astype(jnp.float32)
    pad = jnp.zeros((7, cells_y), jnp.float32)
    msg_xlo = jnp.concatenate([e_x31.reshape(rows, cells_y), regf[cells_x - 1][None], pad], axis=0)
    got_xlo = shifted(msg_xlo, grid, sizes, (1, 0))
    xhi = shifted(e_x0, grid, sizes, (-1, 0))
    ylo = shifted(e_c127, grid, sizes, (0, 1))
    yhi = shifted(e_c0, grid, sizes, (0, -1))
    reg_ycol = shifted(region[:, cells_y - 1:cells_y], grid, sizes, (0, 1))
    c1 = shifted(e_c0[cells_x - 1:cells_x], grid, sizes, (1, -1))
    c2 = shifted(e_c127[0:1], grid, sizes, (-1, 1))

    xlo = got_xlo[:rows].reshape(planes, samples_dev, cells_y)
    reg_xlo = got_xlo[rows:rows + 1].astype(jnp.int32)

    onehot = (level_index[:, None] == lax.iota(jnp.int32, reluctivity.shape[0])[None, :]).astype(jnp.float32)
    base_rows = jnp.sum(onehot[:, :, None] * reluctivity[None], axis=1)
    tile_sample = jnp.minimum(lax.iota(jnp.int32, cells_y) // planes, samples_dev - 1)
    bt = base_rows[tile_sample].T

    resid = residual(potential, source, xlo, xhi, ylo, yhi, e_c0, c2, bt, c1, base_rows, saturation,
                     region, reg_xlo, reg_ycol)

    sample_ids = me_tm * samples_dev + lax.iota(jnp.int32, samples_dev)
    tabs = [
        fourier_rows(((me_tm + d) % n_tm) * q_dev + lax.iota(jnp.int32, q_dev), sample_ids, sample_count)
        for d in range(n_tm)
    ]
    row_last = info_all[:, :cells_x].reshape(n_tm, q_dev, cells_x)
    parts = [jnp.einsum("qs,psxy->qpxy", tabs[d], resid, precision=lax.Precision.HIGHEST) for d in range(n_tm)]
    got_parts = [
        lax.ppermute(parts[d], "tm", [(i, (i + d) % n_tm) for i in range(n_tm)]) for d in range(1, n_tm)
    ]
    tails = jnp.concatenate(
        [jnp.einsum("qb,qpby->qpy", row_last[d], parts[d], precision=lax.Precision.HIGHEST) for d in range(n_tm)],
        axis=0,
    )
    msg_tail = jnp.concatenate([tails, jnp.broadcast_to(gain_all[:, None, None], (n_tm * q_dev, 1, cells_y))], axis=1)
    carried = jnp.zeros_like(tails)
    for d in range(n_gx - 1, 0, -1):
        got = lax.ppermute(msg_tail, "gx", [(i, i + d) for i in range(n_gx - d)])
        stepped = got[:, :planes] + got[:, planes:planes + 1] * carried
        carried = jnp.where(me_gx >= d, stepped, carried)
    carried = carried.reshape(n_tm, q_dev, planes, cells_y)
    got_carried = [
        lax.ppermute(carried[d], "tm", [(i, (i + d) % n_tm) for i in range(n_tm)]) for d in range(1, n_tm)
    ]
    spectrum = parts[0]
    for got in got_parts:
        spectrum = spectrum + got
    carried_own = carried[0]
    for got in got_carried:
        carried_own = carried_own + got
    solved = jnp.einsum("qab,qpby->qpay", inverse, spectrum, precision=lax.Precision.HIGHEST)
    injected = transmit[:, 0][:, None, None] * carried_own
    return solved + injected[:, :, None, :] * inverse[:, :, 0][:, None, :, None]


def solution(mesh):
    in_specs = (
        P("tm", None, "gx", "gy"),
        P("tm", None, "gx", "gy"),
        P("gx", "gy"),
        P("tm"),
        P(),
        P(),
        P("tm", "gx", None),
        P("tm", "gx"),
    )
    out_specs = P("tm", None, "gx", "gy")
    return jax.shard_map(local, mesh=mesh, in_specs=in_specs, out_specs=out_specs, check_vma=False)
```

```python
import functools
import math

import jax
import jax.numpy as jnp
from jax import lax
from jax.experimental import pallas as pl
from jax.experimental.pallas import tpu as pltpu
from jax.sharding import PartitionSpec as P

axial_coupling = 0.5
SAMPLE_BLOCK = 8


def shifted(block, axes, sizes, delta):
    route = []
    for i in range(sizes[0]):
        for j in range(sizes[1]):
            si, sj = i - delta[0], j - delta[1]
            if 0 <= si < sizes[0] and 0 <= sj < sizes[1]:
                route.append((si * sizes[1] + sj, i * sizes[1] + j))
    return lax.ppermute(block, axes, route)


def fourier_rows(row_ids, sample_ids, sample_count):
    half_count = sample_count // 2
    harmonic = jnp.where(row_ids <= half_count, row_ids, row_ids - half_count)
    phase_index = harmonic[:, None] * sample_ids[None, :] % sample_count
    angle_value = phase_index.astype(jnp.float32) * (2.0 * math.pi / sample_count)
    dft_table = jnp.where(
        (row_ids <= half_count)[:, None], jnp.cos(angle_value), jnp.sin(angle_value)
    )
    return dft_table * math.sqrt(2.0 / sample_count)


def col_to_row(col, ix, iy):
    full = jnp.broadcast_to(col, ix.shape)
    return jnp.sum(jnp.where(ix == iy, full, 0.0), axis=0, keepdims=True)


def row_to_col(row, ix, iy):
    full = jnp.broadcast_to(row, ix.shape)
    return jnp.sum(jnp.where(ix == iy, full, 0.0), axis=1, keepdims=True)


def edges_kernel(a_ref, reg_ref, xlo_ref, xhi_ref, c127_ref, c0_ref, c1_ref, c2_ref):
    n_s, planes, nx, ny = a_ref.shape
    rows = planes * n_s
    ix = lax.broadcasted_iota(jnp.int32, (nx, ny), 0)
    iy = lax.broadcasted_iota(jnp.int32, (nx, ny), 1)
    regf = reg_ref[...].astype(jnp.float32)
    xlo_ref[pl.ds(rows, 8), :] = jnp.zeros((8, ny), jnp.float32)
    xlo_ref[pl.ds(rows, 1), :] = regf[nx - 1:nx, :]
    c127_ref[pl.ds(nx, 8), :] = jnp.zeros((8, ny), jnp.float32)
    c127_ref[pl.ds(nx, 1), :] = col_to_row(regf[:, ny - 1:ny], ix, iy)

    def body(s, carry):
        acc127, acc0 = carry
        for p in range(planes):
            t = s * planes + p
            a = a_ref[s, p]
            xlo_ref[pl.ds(p * n_s + s, 1), :] = a[nx - 1:nx, :]
            xhi_ref[pl.ds(p * n_s + s, 1), :] = a[0:1, :]
            acc127 = jnp.where(iy == t, pltpu.roll(a, lax.rem(t + 1, ny), 1), acc127)
            acc0 = jnp.where(iy == t, pltpu.roll(a, t, 1), acc0)
        return acc127, acc0

    zero = jnp.zeros((nx, ny), jnp.float32)
    acc127, acc0 = lax.fori_loop(0, n_s, body, (zero, zero))
    c127_ref[pl.ds(0, nx), :] = acc127
    c0_ref[...] = acc0
    c1_ref[...] = acc0[nx - 1:nx, :]
    c2_ref[...] = acc127[0:1, :]


def edges(a, region):
    n_s, planes, nx, ny = a.shape
    rows = planes * n_s
    vmem = pl.BlockSpec(memory_space=pltpu.VMEM)
    f32 = jnp.float32
    shapes = [
        jax.ShapeDtypeStruct((rows + 8, ny), f32),
        jax.ShapeDtypeStruct((rows, ny), f32),
        jax.ShapeDtypeStruct((nx + 8, ny), f32),
        jax.ShapeDtypeStruct((nx, ny), f32),
        jax.ShapeDtypeStruct((1, ny), f32),
        jax.ShapeDtypeStruct((1, ny), f32),
    ]
    return pl.pallas_call(
        edges_kernel,
        in_specs=[vmem, vmem],
        out_specs=[vmem] * 6,
        out_shape=shapes,
        name="halo_edges",
    )(a, region)


def residual_kernel(kinds, levels, a_ref, src_ref, xlo_ref, xhi_ref, ylo_ref, yhi_ref, own0_ref, c2_ref,
                    c1_ref, level_ref, relu_ref, sat_ref, reg_ref, out_ref):
    blk = pl.program_id(0)
    n_s, planes, nx, ny = a_ref.shape
    n_all = n_s * pl.num_programs(0)
    rows = planes * n_all
    ix = lax.broadcasted_iota(jnp.int32, (nx, ny), 0)
    iy = lax.broadcasted_iota(jnp.int32, (nx, ny), 1)
    iy_row = lax.broadcasted_iota(jnp.int32, (1, ny), 1)
    reg = reg_ref[...]
    reg_xlo = xlo_ref[pl.ds(rows, 1), :].astype(jnp.int32)
    reg_ycol = row_to_col(ylo_ref[pl.ds(nx, 1), :], ix, iy).astype(jnp.int32)

    def lookup(kind, pick):
        out = jnp.broadcast_to(pick(0), kind.shape).astype(jnp.float32)
        for k in range(1, kinds):
            out = jnp.where(kind == k, pick(k), out)
        return out

    sat = lookup(reg, lambda k: sat_ref[k])
    sat_xlo = lookup(reg_xlo, lambda k: sat_ref[k])
    lane_sample = iy_row // planes
    lane_level = jnp.zeros((1, ny), jnp.int32)
    for s in range(n_all):
        lane_level = jnp.where(lane_sample == s, level_ref[s], lane_level)
    bt = []
    for k in range(kinds):
        row = jnp.full((1, ny), relu_ref[0, k], jnp.float32)
        for lv in range(1, levels):
            row = jnp.where(lane_level == lv, relu_ref[lv, k], row)
        bt.append(row)
    c_lo = ylo_ref[pl.ds(0, nx), :]
    lo_xp = jnp.where(ix == nx - 1, c2_ref[...], pltpu.roll(c_lo, nx - 1, 0))
    sx_c = lo_xp - c_lo
    sy_c = own0_ref[...] - c_lo
    kind_c = jnp.broadcast_to(reg_ycol, (nx, ny))
    base_c = lookup(kind_c, lambda k: bt[k])
    sat_c = lookup(kind_c, lambda k: sat_ref[k])
    fy_cols = base_c * (1.0 + sat_c * (sx_c * sx_c + sy_c * sy_c)) * sy_c
    c_hi = yhi_ref[...]

    def body(s, carry):
        s_glob = blk * n_s + s
        lv = level_ref[s_glob]
        base = lookup(reg, lambda k: relu_ref[lv, k])
        base_xlo = lookup(reg_xlo, lambda k: relu_ref[lv, k])
        tiles = [a_ref[s, p] for p in range(planes)]
        for p in range(planes):
            t = s_glob * planes + p
            a = tiles[p]
            row_hi = xhi_ref[pl.ds(p * n_all + s_glob, 1), :]
            row_lo = xlo_ref[pl.ds(p * n_all + s_glob, 1), :]
            c1 = c1_ref[0, t]
            col_hi = pltpu.roll(c_hi, lax.rem(ny - 1 - t + ny, ny), 1)
            a_xp = jnp.where(ix == nx - 1, row_hi, pltpu.roll(a, nx - 1, 0))
            a_yp = jnp.where(iy == ny - 1, col_hi, pltpu.roll(a, ny - 1, 1))
            sx = a_xp - a
            sy = a_yp - a
            rel = base * (1.0 + sat * (sx * sx + sy * sy))
            fx = rel * sx
            fy = rel * sy
            lo_yp = jnp.where(iy_row == ny - 1, c1, pltpu.roll(row_lo, ny - 1, 1))
            sx_l = a[0:1, :] - row_lo
            sy_l = lo_yp - row_lo
            fx_l = base_xlo * (1.0 + sat_xlo * (sx_l * sx_l + sy_l * sy_l)) * sx_l
            fy_c = pltpu.roll(fy_cols, lax.rem(ny - t, ny), 1)
            fx_down = jnp.where(ix == 0, fx_l, pltpu.roll(fx, 1, 0))
            fy_left = jnp.where(iy == 0, fy_c, pltpu.roll(fy, 1, 1))
            curl = fx_down - fx + fy_left - fy
            axial = 2.0 * a
            if p > 0:
                axial = axial - tiles[p - 1]
            if p < planes - 1:
                axial = axial - tiles[p + 1]
            out_ref[p, s] = curl + axial_coupling * axial - src_ref[s, p]
        return carry

    lax.fori_loop(0, n_s, body, 0)


def residual(a, src, xlo, xhi, ylo, yhi, own0, c2, c1, level_index, reluctivity, saturation, reg):
    n_s, planes, nx, ny = a.shape
    levels, kinds = reluctivity.shape
    sb = min(SAMPLE_BLOCK, n_s)
    tile = pl.BlockSpec((sb, planes, nx, ny), lambda i: (i, 0, 0, 0))
    vmem_whole = pl.BlockSpec(memory_space=pltpu.VMEM)
    smem_whole = pl.BlockSpec(memory_space=pltpu.SMEM)
    return pl.pallas_call(
        functools.partial(residual_kernel, kinds, levels),
        grid=(n_s // sb,),
        in_specs=[tile, tile] + [vmem_whole] * 6 + [smem_whole] * 4 + [vmem_whole],
        out_specs=pl.BlockSpec((planes, sb, nx, ny), lambda i: (0, i, 0, 0)),
        out_shape=jax.ShapeDtypeStruct((planes, n_s, nx, ny), jnp.float32),
        name="residual",
    )(a, src, xlo, xhi, ylo, yhi, own0, c2, c1, level_index, reluctivity, saturation, reg)


def local(potential, source, region, level_index, reluctivity, saturation, inverse, transmit):
    samples_dev, planes, cells_x, cells_y = potential.shape
    n_tm = lax.axis_size("tm")
    n_gx = lax.axis_size("gx")
    n_gy = lax.axis_size("gy")
    me_tm = lax.axis_index("tm")
    me_gx = lax.axis_index("gx")
    sample_count = samples_dev * n_tm
    q_dev = samples_dev
    grid = ("gx", "gy")
    sizes = (n_gx, n_gy)
    rows = planes * samples_dev

    gain_here = transmit[:, 0] * inverse[:, cells_x - 1, 0]
    own_info = jnp.concatenate([inverse[:, cells_x - 1, :], gain_here[:, None]], axis=1)
    infos = [own_info]
    for d in range(1, n_tm):
        infos.append(lax.ppermute(own_info, "tm", [(i, (i - d) % n_tm) for i in range(n_tm)]))
    info_all = jnp.concatenate(infos, axis=0)
    gain_all = info_all[:, cells_x]

    msg_xlo, msg_xhi, msg_c127, msg_c0, msg_c1, msg_c2 = edges(potential, region)
    xlo = shifted(msg_xlo, grid, sizes, (1, 0))
    xhi = shifted(msg_xhi, grid, sizes, (-1, 0))
    ylo = shifted(msg_c127, grid, sizes, (0, 1))
    yhi = shifted(msg_c0, grid, sizes, (0, -1))
    c1 = shifted(msg_c1, grid, sizes, (1, -1))
    c2 = shifted(msg_c2, grid, sizes, (-1, 1))
    resid = residual(potential, source, xlo, xhi, ylo, yhi, msg_c0, c2, c1, level_index, reluctivity,
                     saturation, region)

    sample_ids = me_tm * samples_dev + lax.iota(jnp.int32, samples_dev)
    tabs = [
        fourier_rows(((me_tm + d) % n_tm) * q_dev + lax.iota(jnp.int32, q_dev), sample_ids, sample_count)
        for d in range(n_tm)
    ]
    row_last = info_all[:, :cells_x].reshape(n_tm, q_dev, cells_x)
    parts = [jnp.einsum("qs,psxy->qpxy", tabs[d], resid, precision=lax.Precision.HIGHEST) for d in range(n_tm)]
    got_parts = [
        lax.ppermute(parts[d], "tm", [(i, (i + d) % n_tm) for i in range(n_tm)]) for d in range(1, n_tm)
    ]
    tails = jnp.concatenate(
        [jnp.einsum("qb,qpby->qpy", row_last[d], parts[d], precision=lax.Precision.HIGHEST) for d in range(n_tm)],
        axis=0,
    )
    msg_tail = jnp.concatenate([tails, jnp.broadcast_to(gain_all[:, None, None], (n_tm * q_dev, 1, cells_y))], axis=1)
    carried = jnp.zeros_like(tails)
    for d in range(n_gx - 1, 0, -1):
        got = lax.ppermute(msg_tail, "gx", [(i, i + d) for i in range(n_gx - d)])
        stepped = got[:, :planes] + got[:, planes:planes + 1] * carried
        carried = jnp.where(me_gx >= d, stepped, carried)
    carried = carried.reshape(n_tm, q_dev, planes, cells_y)
    got_carried = [
        lax.ppermute(carried[d], "tm", [(i, (i + d) % n_tm) for i in range(n_tm)]) for d in range(1, n_tm)
    ]
    spectrum = parts[0]
    for got in got_parts:
        spectrum = spectrum + got
    carried_own = carried[0]
    for got in got_carried:
        carried_own = carried_own + got
    solved = jnp.einsum("qab,qpby->qpay", inverse, spectrum, precision=lax.Precision.HIGHEST)
    injected = transmit[:, 0][:, None, None] * carried_own
    return solved + injected[:, :, None, :] * inverse[:, :, 0][:, None, :, None]


def solution(mesh):
    in_specs = (
        P("tm", None, "gx", "gy"),
        P("tm", None, "gx", "gy"),
        P("gx", "gy"),
        P("tm"),
        P(),
        P(),
        P("tm", "gx", None),
        P("tm", "gx"),
    )
    out_specs = P("tm", None, "gx", "gy")
    return jax.shard_map(local, mesh=mesh, in_specs=in_specs, out_specs=out_specs, check_vma=False)
```

```python
import functools
import math

import jax
import jax.numpy as jnp
from jax import lax
from jax.experimental import pallas as pl
from jax.experimental.pallas import tpu as pltpu
from jax.sharding import PartitionSpec as P

axial_coupling = 0.5
SAMPLE_BLOCK = 8


def shifted(block, axes, sizes, delta):
    route = []
    for i in range(sizes[0]):
        for j in range(sizes[1]):
            si, sj = i - delta[0], j - delta[1]
            if 0 <= si < sizes[0] and 0 <= sj < sizes[1]:
                route.append((si * sizes[1] + sj, i * sizes[1] + j))
    return lax.ppermute(block, axes, route)


def fourier_rows(row_ids, sample_ids, sample_count):
    half_count = sample_count // 2
    harmonic = jnp.where(row_ids <= half_count, row_ids, row_ids - half_count)
    phase_index = harmonic[:, None] * sample_ids[None, :] % sample_count
    angle_value = phase_index.astype(jnp.float32) * (2.0 * math.pi / sample_count)
    dft_table = jnp.where(
        (row_ids <= half_count)[:, None], jnp.cos(angle_value), jnp.sin(angle_value)
    )
    return dft_table * math.sqrt(2.0 / sample_count)


def col_to_row(col, ix, iy):
    full = jnp.broadcast_to(col, ix.shape)
    return jnp.sum(jnp.where(ix == iy, full, 0.0), axis=0, keepdims=True)


def row_to_col(row, ix, iy):
    full = jnp.broadcast_to(row, ix.shape)
    return jnp.sum(jnp.where(ix == iy, full, 0.0), axis=1, keepdims=True)


def edges_kernel(a_ref, reg_ref, xlo_ref, xhi_ref, c127_ref, c0_ref, c1_ref, c2_ref):
    n_s, planes, nx, ny = a_ref.shape
    rows = planes * n_s
    ix = lax.broadcasted_iota(jnp.int32, (nx, ny), 0)
    iy = lax.broadcasted_iota(jnp.int32, (nx, ny), 1)
    regf = reg_ref[...].astype(jnp.float32)
    xlo_ref[pl.ds(rows, 8), :] = jnp.zeros((8, ny), jnp.float32)
    xlo_ref[pl.ds(rows, 1), :] = regf[nx - 1:nx, :]
    c127_ref[pl.ds(nx, 8), :] = jnp.zeros((8, ny), jnp.float32)
    c127_ref[pl.ds(nx, 1), :] = col_to_row(regf[:, ny - 1:ny], ix, iy)

    def body(s, carry):
        acc127, acc0 = carry
        for p in range(planes):
            t = s * planes + p
            a = a_ref[s, p]
            xlo_ref[pl.ds(p * n_s + s, 1), :] = a[nx - 1:nx, :]
            xhi_ref[pl.ds(p * n_s + s, 1), :] = a[0:1, :]
            acc127 = jnp.where(iy == t, pltpu.roll(a, lax.rem(t + 1, ny), 1), acc127)
            acc0 = jnp.where(iy == t, pltpu.roll(a, t, 1), acc0)
        return acc127, acc0

    zero = jnp.zeros((nx, ny), jnp.float32)
    acc127, acc0 = lax.fori_loop(0, n_s, body, (zero, zero))
    c127_ref[pl.ds(0, nx), :] = acc127
    c0_ref[...] = acc0
    c1_ref[...] = acc0[nx - 1:nx, :]
    c2_ref[...] = acc127[0:1, :]


def edges(a, region):
    n_s, planes, nx, ny = a.shape
    rows = planes * n_s
    vmem = pl.BlockSpec(memory_space=pltpu.VMEM)
    f32 = jnp.float32
    shapes = [
        jax.ShapeDtypeStruct((rows + 8, ny), f32),
        jax.ShapeDtypeStruct((rows, ny), f32),
        jax.ShapeDtypeStruct((nx + 8, ny), f32),
        jax.ShapeDtypeStruct((nx, ny), f32),
        jax.ShapeDtypeStruct((1, ny), f32),
        jax.ShapeDtypeStruct((1, ny), f32),
    ]
    return pl.pallas_call(
        edges_kernel,
        in_specs=[vmem, vmem],
        out_specs=[vmem] * 6,
        out_shape=shapes,
        name="halo_edges",
    )(a, region)


def residual_kernel(kinds, levels, halo, *refs):
    if halo:
        (a_ref, src_ref, xlo_ref, xhi_ref, ylo_ref, yhi_ref, own0_ref, c2_ref,
         c1_ref, level_ref, relu_ref, sat_ref, reg_ref, out_ref) = refs
    else:
        a_ref, src_ref, level_ref, relu_ref, sat_ref, reg_ref, out_ref = refs
    blk = pl.program_id(0)
    n_s, planes, nx, ny = a_ref.shape
    n_all = n_s * pl.num_programs(0)
    rows = planes * n_all
    ix = lax.broadcasted_iota(jnp.int32, (nx, ny), 0)
    iy = lax.broadcasted_iota(jnp.int32, (nx, ny), 1)
    iy_row = lax.broadcasted_iota(jnp.int32, (1, ny), 1)
    reg = reg_ref[...]
    if halo:
        reg_xlo = xlo_ref[pl.ds(rows, 1), :].astype(jnp.int32)
    else:
        reg_xlo = jnp.zeros((1, ny), jnp.int32)

    def lookup(kind, pick):
        out = jnp.broadcast_to(pick(0), kind.shape).astype(jnp.float32)
        for k in range(1, kinds):
            out = jnp.where(kind == k, pick(k), out)
        return out

    sat = lookup(reg, lambda k: sat_ref[k])
    sat_xlo = lookup(reg_xlo, lambda k: sat_ref[k])
    if halo:
        reg_ycol = row_to_col(ylo_ref[pl.ds(nx, 1), :], ix, iy).astype(jnp.int32)
        lane_sample = iy_row // planes
        lane_level = jnp.zeros((1, ny), jnp.int32)
        for s in range(n_all):
            lane_level = jnp.where(lane_sample == s, level_ref[s], lane_level)
        bt = []
        for k in range(kinds):
            row = jnp.full((1, ny), relu_ref[0, k], jnp.float32)
            for lv in range(1, levels):
                row = jnp.where(lane_level == lv, relu_ref[lv, k], row)
            bt.append(row)
        c_lo = ylo_ref[pl.ds(0, nx), :]
        lo_xp = jnp.where(ix == nx - 1, c2_ref[...], pltpu.roll(c_lo, nx - 1, 0))
        sx_c = lo_xp - c_lo
        sy_c = own0_ref[...] - c_lo
        kind_c = jnp.broadcast_to(reg_ycol, (nx, ny))
        base_c = lookup(kind_c, lambda k: bt[k])
        sat_c = lookup(kind_c, lambda k: sat_ref[k])
        fy_cols = base_c * (1.0 + sat_c * (sx_c * sx_c + sy_c * sy_c)) * sy_c
        c_hi = yhi_ref[...]
    zero_row = jnp.zeros((1, ny), jnp.float32)
    zero_tile = jnp.zeros((nx, ny), jnp.float32)

    def body(s, carry):
        s_glob = blk * n_s + s
        lv = level_ref[s_glob]
        base = lookup(reg, lambda k: relu_ref[lv, k])
        base_xlo = lookup(reg_xlo, lambda k: relu_ref[lv, k])
        tiles = [a_ref[s, p] for p in range(planes)]
        for p in range(planes):
            t = s_glob * planes + p
            a = tiles[p]
            if halo:
                row_hi = xhi_ref[pl.ds(p * n_all + s_glob, 1), :]
                row_lo = xlo_ref[pl.ds(p * n_all + s_glob, 1), :]
                c1 = c1_ref[0, t]
                col_hi = pltpu.roll(c_hi, lax.rem(ny - 1 - t + ny, ny), 1)
                fy_c = pltpu.roll(fy_cols, lax.rem(ny - t, ny), 1)
            else:
                row_hi = zero_row
                row_lo = zero_row
                c1 = 0.0
                col_hi = zero_tile
                fy_c = zero_tile
            a_xp = jnp.where(ix == nx - 1, row_hi, pltpu.roll(a, nx - 1, 0))
            a_yp = jnp.where(iy == ny - 1, col_hi, pltpu.roll(a, ny - 1, 1))
            sx = a_xp - a
            sy = a_yp - a
            rel = base * (1.0 + sat * (sx * sx + sy * sy))
            fx = rel * sx
            fy = rel * sy
            lo_yp = jnp.where(iy_row == ny - 1, c1, pltpu.roll(row_lo, ny - 1, 1))
            sx_l = a[0:1, :] - row_lo
            sy_l = lo_yp - row_lo
            fx_l = base_xlo * (1.0 + sat_xlo * (sx_l * sx_l + sy_l * sy_l)) * sx_l
            fx_down = jnp.where(ix == 0, fx_l, pltpu.roll(fx, 1, 0))
            fy_left = jnp.where(iy == 0, fy_c, pltpu.roll(fy, 1, 1))
            curl = fx_down - fx + fy_left - fy
            axial = 2.0 * a
            if p > 0:
                axial = axial - tiles[p - 1]
            if p < planes - 1:
                axial = axial - tiles[p + 1]
            out_ref[p, s] = curl + axial_coupling * axial - src_ref[s, p]
        return carry

    lax.fori_loop(0, n_s, body, 0)


def residual(a, src, halos, level_index, reluctivity, saturation, reg):
    n_s, planes, nx, ny = a.shape
    levels, kinds = reluctivity.shape
    sb = min(SAMPLE_BLOCK, n_s)
    tile = pl.BlockSpec((sb, planes, nx, ny), lambda i: (i, 0, 0, 0))
    vmem_whole = pl.BlockSpec(memory_space=pltpu.VMEM)
    smem_whole = pl.BlockSpec(memory_space=pltpu.SMEM)
    return pl.pallas_call(
        functools.partial(residual_kernel, kinds, levels, halos is not None),
        grid=(n_s // sb,),
        in_specs=[tile, tile] + ([vmem_whole] * 6 + [smem_whole] if halos else []) + [smem_whole] * 3 + [vmem_whole],
        out_specs=pl.BlockSpec((planes, sb, nx, ny), lambda i: (0, i, 0, 0)),
        out_shape=jax.ShapeDtypeStruct((planes, n_s, nx, ny), jnp.float32),
        name="residual",
    )(a, src, *(halos or ()), level_index, reluctivity, saturation, reg)


def local(potential, source, region, level_index, reluctivity, saturation, inverse, transmit):
    samples_dev, planes, cells_x, cells_y = potential.shape
    n_tm = lax.axis_size("tm")
    n_gx = lax.axis_size("gx")
    n_gy = lax.axis_size("gy")
    me_tm = lax.axis_index("tm")
    me_gx = lax.axis_index("gx")
    sample_count = samples_dev * n_tm
    q_dev = samples_dev
    grid = ("gx", "gy")
    sizes = (n_gx, n_gy)
    rows = planes * samples_dev

    gain_here = transmit[:, 0] * inverse[:, cells_x - 1, 0]
    own_info = jnp.concatenate([inverse[:, cells_x - 1, :], gain_here[:, None]], axis=1)
    infos = [own_info]
    for d in range(1, n_tm):
        infos.append(lax.ppermute(own_info, "tm", [(i, (i - d) % n_tm) for i in range(n_tm)]))
    info_all = jnp.concatenate(infos, axis=0)
    gain_all = info_all[:, cells_x]

    sample_ids = me_tm * samples_dev + lax.iota(jnp.int32, samples_dev)
    tabs = [
        fourier_rows(((me_tm + d) % n_tm) * q_dev + lax.iota(jnp.int32, q_dev), sample_ids, sample_count)
        for d in range(n_tm)
    ]
    resid0 = residual(potential, source, None, level_index, reluctivity, saturation, region)
    parts = [jnp.einsum("qs,psxy->qpxy", tabs[d], resid0, precision=lax.Precision.HIGHEST) for d in range(n_tm)]
    got_parts = [
        lax.ppermute(parts[d], "tm", [(i, (i + d) % n_tm) for i in range(n_tm)]) for d in range(1, n_tm)
    ]

    msg_xlo, msg_xhi, msg_c127, msg_c0, msg_c1, msg_c2 = edges(potential, region)
    xlo = shifted(msg_xlo, grid, sizes, (1, 0))
    xhi = shifted(msg_xhi, grid, sizes, (-1, 0))
    ylo = shifted(msg_c127, grid, sizes, (0, 1))
    yhi = shifted(msg_c0, grid, sizes, (0, -1))
    c1 = shifted(msg_c1, grid, sizes, (1, -1))
    c2 = shifted(msg_c2, grid, sizes, (-1, 1))
    resid1 = residual(potential, source, (xlo, xhi, ylo, yhi, msg_c0, c2, c1), level_index, reluctivity,
                      saturation, region)
    delta = resid1 - resid0
    d_rows = jnp.stack([delta[:, :, 0], delta[:, :, cells_x - 1]], axis=2)
    d_cols = jnp.stack([delta[:, :, 1:cells_x - 1, 0], delta[:, :, 1:cells_x - 1, cells_y - 1]], axis=3)
    fix_rows = [jnp.einsum("qs,psry->qpry", tabs[d], d_rows, precision=lax.Precision.HIGHEST) for d in range(n_tm)]
    fix_cols = [jnp.einsum("qs,psxc->qpxc", tabs[d], d_cols, precision=lax.Precision.HIGHEST) for d in range(n_tm)]
    n_row = planes * 2 * cells_y
    fix_msg = [jnp.concatenate([fix_rows[d].reshape(q_dev, -1), fix_cols[d].reshape(q_dev, -1)], axis=1)
               for d in range(n_tm)]
    got_fix = [
        lax.ppermute(fix_msg[d], "tm", [(i, (i + d) % n_tm) for i in range(n_tm)]) for d in range(1, n_tm)
    ]
    xi = lax.broadcasted_iota(jnp.int32, (1, 1, cells_x, cells_y), 2)
    yi = lax.broadcasted_iota(jnp.int32, (1, 1, cells_x, cells_y), 3)

    def expand(msg):
        r = msg[:, :n_row].reshape(q_dev, planes, 2, cells_y)
        c = jnp.pad(msg[:, n_row:].reshape(q_dev, planes, cells_x - 2, 2), ((0, 0), (0, 0), (1, 1), (0, 0)))
        out = jnp.where(yi == cells_y - 1, c[..., 1:2], 0.0)
        out = jnp.where(yi == 0, c[..., 0:1], out)
        out = jnp.where(xi == cells_x - 1, r[:, :, 1:2], out)
        return jnp.where(xi == 0, r[:, :, 0:1], out)

    true_parts = [parts[d] + expand(fix_msg[d]) for d in range(n_tm)]
    row_last = info_all[:, :cells_x].reshape(n_tm, q_dev, cells_x)
    tails = jnp.concatenate(
        [jnp.einsum("qb,qpby->qpy", row_last[d], true_parts[d], precision=lax.Precision.HIGHEST)
         for d in range(n_tm)],
        axis=0,
    )
    msg_tail = jnp.concatenate([tails, jnp.broadcast_to(gain_all[:, None, None], (n_tm * q_dev, 1, cells_y))], axis=1)
    carried = jnp.zeros_like(tails)
    for d in range(n_gx - 1, 0, -1):
        got = lax.ppermute(msg_tail, "gx", [(i, i + d) for i in range(n_gx - d)])
        stepped = got[:, :planes] + got[:, planes:planes + 1] * carried
        carried = jnp.where(me_gx >= d, stepped, carried)
    carried = carried.reshape(n_tm, q_dev, planes, cells_y)
    got_carried = [
        lax.ppermute(carried[d], "tm", [(i, (i + d) % n_tm) for i in range(n_tm)]) for d in range(1, n_tm)
    ]
    spectrum = true_parts[0]
    for got, fix in zip(got_parts, got_fix):
        spectrum = spectrum + (got + expand(fix))
    carried_own = carried[0]
    for got in got_carried:
        carried_own = carried_own + got
    solved = jnp.einsum("qab,qpby->qpay", inverse, spectrum, precision=lax.Precision.HIGHEST)
    injected = transmit[:, 0][:, None, None] * carried_own
    return solved + injected[:, :, None, :] * inverse[:, :, 0][:, None, :, None]


def solution(mesh):
    in_specs = (
        P("tm", None, "gx", "gy"),
        P("tm", None, "gx", "gy"),
        P("gx", "gy"),
        P("tm"),
        P(),
        P(),
        P("tm", "gx", None),
        P("tm", "gx"),
    )
    out_specs = P("tm", None, "gx", "gy")
    return jax.shard_map(local, mesh=mesh, in_specs=in_specs, out_specs=out_specs, check_vma=False)
```

```python
import functools
import math

import jax
import jax.numpy as jnp
from jax import lax
from jax.experimental import pallas as pl
from jax.experimental.pallas import tpu as pltpu
from jax.sharding import PartitionSpec as P

axial_coupling = 0.5
SAMPLE_BLOCK = 8


def shifted(block, axes, sizes, delta):
    route = []
    for i in range(sizes[0]):
        for j in range(sizes[1]):
            si, sj = i - delta[0], j - delta[1]
            if 0 <= si < sizes[0] and 0 <= sj < sizes[1]:
                route.append((si * sizes[1] + sj, i * sizes[1] + j))
    return lax.ppermute(block, axes, route)


def fourier_rows(row_ids, sample_ids, sample_count):
    half_count = sample_count // 2
    harmonic = jnp.where(row_ids <= half_count, row_ids, row_ids - half_count)
    phase_index = harmonic[:, None] * sample_ids[None, :] % sample_count
    angle_value = phase_index.astype(jnp.float32) * (2.0 * math.pi / sample_count)
    dft_table = jnp.where(
        (row_ids <= half_count)[:, None], jnp.cos(angle_value), jnp.sin(angle_value)
    )
    return dft_table * math.sqrt(2.0 / sample_count)


def col_to_row(col, ix, iy):
    full = jnp.broadcast_to(col, ix.shape)
    return jnp.sum(jnp.where(ix == iy, full, 0.0), axis=0, keepdims=True)


def row_to_col(row, ix, iy):
    full = jnp.broadcast_to(row, ix.shape)
    return jnp.sum(jnp.where(ix == iy, full, 0.0), axis=1, keepdims=True)


def edges_kernel(a_ref, reg_ref, xlo_ref, xhi_ref, c127_ref, c0_ref, c1_ref, c2_ref):
    n_s, planes, nx, ny = a_ref.shape
    rows = planes * n_s
    ix = lax.broadcasted_iota(jnp.int32, (nx, ny), 0)
    iy = lax.broadcasted_iota(jnp.int32, (nx, ny), 1)
    regf = reg_ref[...].astype(jnp.float32)
    xlo_ref[pl.ds(rows, 8), :] = jnp.zeros((8, ny), jnp.float32)
    xlo_ref[pl.ds(rows, 1), :] = regf[nx - 1:nx, :]
    c127_ref[pl.ds(nx, 8), :] = jnp.zeros((8, ny), jnp.float32)
    c127_ref[pl.ds(nx, 1), :] = col_to_row(regf[:, ny - 1:ny], ix, iy)

    acc127 = jnp.zeros((nx, ny), jnp.float32)
    acc0 = jnp.zeros((nx, ny), jnp.float32)
    for s in range(n_s):
        for p in range(planes):
            t = s * planes + p
            a = a_ref[s, p]
            xlo_ref[pl.ds(p * n_s + s, 1), :] = a[nx - 1:nx, :]
            xhi_ref[pl.ds(p * n_s + s, 1), :] = a[0:1, :]
            acc127 = jnp.where(iy == t, pltpu.roll(a, (t + 1) % ny, 1), acc127)
            acc0 = jnp.where(iy == t, a if t == 0 else pltpu.roll(a, t, 1), acc0)
    c127_ref[pl.ds(0, nx), :] = acc127
    c0_ref[...] = acc0
    c1_ref[...] = acc0[nx - 1:nx, :]
    c2_ref[...] = acc127[0:1, :]


def edges(a, region):
    n_s, planes, nx, ny = a.shape
    rows = planes * n_s
    vmem = pl.BlockSpec(memory_space=pltpu.VMEM)
    f32 = jnp.float32
    shapes = [
        jax.ShapeDtypeStruct((rows + 8, ny), f32),
        jax.ShapeDtypeStruct((rows, ny), f32),
        jax.ShapeDtypeStruct((nx + 8, ny), f32),
        jax.ShapeDtypeStruct((nx, ny), f32),
        jax.ShapeDtypeStruct((1, ny), f32),
        jax.ShapeDtypeStruct((1, ny), f32),
    ]
    return pl.pallas_call(
        edges_kernel,
        in_specs=[vmem, vmem],
        out_specs=[vmem] * 6,
        out_shape=shapes,
        name="halo_edges",
    )(a, region)


def residual_kernel(kinds, levels, a_ref, src_ref, xlo_ref, xhi_ref, ylo_ref, yhi_ref, own0_ref, c2_ref,
                    c1_ref, level_ref, relu_ref, sat_ref, reg_ref, out_ref):
    blk = pl.program_id(0)
    n_s, planes, nx, ny = a_ref.shape
    n_all = n_s * pl.num_programs(0)
    rows = planes * n_all
    ix = lax.broadcasted_iota(jnp.int32, (nx, ny), 0)
    iy = lax.broadcasted_iota(jnp.int32, (nx, ny), 1)
    iy_row = lax.broadcasted_iota(jnp.int32, (1, ny), 1)
    reg = reg_ref[...]
    reg_xlo = xlo_ref[pl.ds(rows, 1), :].astype(jnp.int32)
    reg_ycol = row_to_col(ylo_ref[pl.ds(nx, 1), :], ix, iy).astype(jnp.int32)

    def lookup(kind, pick):
        out = jnp.broadcast_to(pick(0), kind.shape).astype(jnp.float32)
        for k in range(1, kinds):
            out = jnp.where(kind == k, pick(k), out)
        return out

    sat = lookup(reg, lambda k: sat_ref[k])
    sat_xlo = lookup(reg_xlo, lambda k: sat_ref[k])
    lane_sample = iy_row // planes
    lane_level = jnp.zeros((1, ny), jnp.int32)
    for s in range(n_all):
        lane_level = jnp.where(lane_sample == s, level_ref[s], lane_level)
    bt = []
    for k in range(kinds):
        row = jnp.full((1, ny), relu_ref[0, k], jnp.float32)
        for lv in range(1, levels):
            row = jnp.where(lane_level == lv, relu_ref[lv, k], row)
        bt.append(row)
    c_lo = ylo_ref[pl.ds(0, nx), :]
    lo_xp = jnp.where(ix == nx - 1, c2_ref[...], pltpu.roll(c_lo, nx - 1, 0))
    sx_c = lo_xp - c_lo
    sy_c = own0_ref[...] - c_lo
    kind_c = jnp.broadcast_to(reg_ycol, (nx, ny))
    base_c = lookup(kind_c, lambda k: bt[k])
    sat_c = lookup(kind_c, lambda k: sat_ref[k])
    fy_cols = base_c * (1.0 + sat_c * (sx_c * sx_c + sy_c * sy_c)) * sy_c
    c_hi = yhi_ref[...]

    def body(s, carry):
        s_glob = blk * n_s + s
        lv = level_ref[s_glob]
        base = lookup(reg, lambda k: relu_ref[lv, k])
        base_xlo = lookup(reg_xlo, lambda k: relu_ref[lv, k])
        tiles = [a_ref[s, p] for p in range(planes)]
        for p in range(planes):
            t = s_glob * planes + p
            a = tiles[p]
            row_hi = xhi_ref[pl.ds(p * n_all + s_glob, 1), :]
            row_lo = xlo_ref[pl.ds(p * n_all + s_glob, 1), :]
            c1 = c1_ref[0, t]
            col_hi = pltpu.roll(c_hi, lax.rem(ny - 1 - t + ny, ny), 1)
            a_xp = jnp.where(ix == nx - 1, row_hi, pltpu.roll(a, nx - 1, 0))
            a_yp = jnp.where(iy == ny - 1, col_hi, pltpu.roll(a, ny - 1, 1))
            sx = a_xp - a
            sy = a_yp - a
            rel = base * (1.0 + sat * (sx * sx + sy * sy))
            fx = rel * sx
            fy = rel * sy
            lo_yp = jnp.where(iy_row == ny - 1, c1, pltpu.roll(row_lo, ny - 1, 1))
            sx_l = a[0:1, :] - row_lo
            sy_l = lo_yp - row_lo
            fx_l = base_xlo * (1.0 + sat_xlo * (sx_l * sx_l + sy_l * sy_l)) * sx_l
            fy_c = pltpu.roll(fy_cols, lax.rem(ny - t, ny), 1)
            fx_down = jnp.where(ix == 0, fx_l, pltpu.roll(fx, 1, 0))
            fy_left = jnp.where(iy == 0, fy_c, pltpu.roll(fy, 1, 1))
            curl = fx_down - fx + fy_left - fy
            axial = 2.0 * a
            if p > 0:
                axial = axial - tiles[p - 1]
            if p < planes - 1:
                axial = axial - tiles[p + 1]
            out_ref[p, s] = curl + axial_coupling * axial - src_ref[s, p]
        return carry

    lax.fori_loop(0, n_s, body, 0)


def residual(a, src, xlo, xhi, ylo, yhi, own0, c2, c1, level_index, reluctivity, saturation, reg):
    n_s, planes, nx, ny = a.shape
    levels, kinds = reluctivity.shape
    sb = min(SAMPLE_BLOCK, n_s)
    tile = pl.BlockSpec((sb, planes, nx, ny), lambda i: (i, 0, 0, 0))
    vmem_whole = pl.BlockSpec(memory_space=pltpu.VMEM)
    smem_whole = pl.BlockSpec(memory_space=pltpu.SMEM)
    return pl.pallas_call(
        functools.partial(residual_kernel, kinds, levels),
        grid=(n_s // sb,),
        in_specs=[tile, tile] + [vmem_whole] * 6 + [smem_whole] * 4 + [vmem_whole],
        out_specs=pl.BlockSpec((planes, sb, nx, ny), lambda i: (0, i, 0, 0)),
        out_shape=jax.ShapeDtypeStruct((planes, n_s, nx, ny), jnp.float32),
        name="residual",
    )(a, src, xlo, xhi, ylo, yhi, own0, c2, c1, level_index, reluctivity, saturation, reg)


def local(potential, source, region, level_index, reluctivity, saturation, inverse, transmit):
    samples_dev, planes, cells_x, cells_y = potential.shape
    n_tm = lax.axis_size("tm")
    n_gx = lax.axis_size("gx")
    n_gy = lax.axis_size("gy")
    me_tm = lax.axis_index("tm")
    me_gx = lax.axis_index("gx")
    sample_count = samples_dev * n_tm
    q_dev = samples_dev
    grid = ("gx", "gy")
    sizes = (n_gx, n_gy)
    rows = planes * samples_dev

    gain_here = transmit[:, 0] * inverse[:, cells_x - 1, 0]
    own_info = jnp.concatenate([inverse[:, cells_x - 1, :], gain_here[:, None]], axis=1)
    infos = [own_info]
    for d in range(1, n_tm):
        infos.append(lax.ppermute(own_info, "tm", [(i, (i - d) % n_tm) for i in range(n_tm)]))
    info_all = jnp.concatenate(infos, axis=0)
    gain_all = info_all[:, cells_x]

    msg_xlo, msg_xhi, msg_c127, msg_c0, msg_c1, msg_c2 = edges(potential, region)
    xlo = shifted(msg_xlo, grid, sizes, (1, 0))
    xhi = shifted(msg_xhi, grid, sizes, (-1, 0))
    ylo = shifted(msg_c127, grid, sizes, (0, 1))
    yhi = shifted(msg_c0, grid, sizes, (0, -1))
    c1 = shifted(msg_c1, grid, sizes, (1, -1))
    c2 = shifted(msg_c2, grid, sizes, (-1, 1))
    resid = residual(potential, source, xlo, xhi, ylo, yhi, msg_c0, c2, c1, level_index, reluctivity,
                     saturation, region)

    sample_ids = me_tm * samples_dev + lax.iota(jnp.int32, samples_dev)
    tabs = [
        fourier_rows(((me_tm + d) % n_tm) * q_dev + lax.iota(jnp.int32, q_dev), sample_ids, sample_count)
        for d in range(n_tm)
    ]
    row_last = info_all[:, :cells_x].reshape(n_tm, q_dev, cells_x)
    parts = [jnp.einsum("qs,psxy->qpxy", tabs[d], resid, precision=lax.Precision.HIGHEST) for d in range(n_tm)]
    got_parts = [
        lax.ppermute(parts[d], "tm", [(i, (i + d) % n_tm) for i in range(n_tm)]) for d in range(1, n_tm)
    ]
    tails = jnp.concatenate(
        [jnp.einsum("qb,qpby->qpy", row_last[d], parts[d], precision=lax.Precision.HIGHEST) for d in range(n_tm)],
        axis=0,
    )
    msg_tail = jnp.concatenate([tails, jnp.broadcast_to(gain_all[:, None, None], (n_tm * q_dev, 1, cells_y))], axis=1)
    carried = jnp.zeros_like(tails)
    for d in range(n_gx - 1, 0, -1):
        got = lax.ppermute(msg_tail, "gx", [(i, i + d) for i in range(n_gx - d)])
        stepped = got[:, :planes] + got[:, planes:planes + 1] * carried
        carried = jnp.where(me_gx >= d, stepped, carried)
    carried = carried.reshape(n_tm, q_dev, planes, cells_y)
    got_carried = [
        lax.ppermute(carried[d], "tm", [(i, (i + d) % n_tm) for i in range(n_tm)]) for d in range(1, n_tm)
    ]
    spectrum = parts[0]
    for got in got_parts:
        spectrum = spectrum + got
    carried_own = carried[0]
    for got in got_carried:
        carried_own = carried_own + got
    solved = jnp.einsum("qab,qpby->qpay", inverse, spectrum, precision=lax.Precision.HIGHEST)
    injected = transmit[:, 0][:, None, None] * carried_own
    return solved + injected[:, :, None, :] * inverse[:, :, 0][:, None, :, None]


def solution(mesh):
    in_specs = (
        P("tm", None, "gx", "gy"),
        P("tm", None, "gx", "gy"),
        P("gx", "gy"),
        P("tm"),
        P(),
        P(),
        P("tm", "gx", None),
        P("tm", "gx"),
    )
    out_specs = P("tm", None, "gx", "gy")
    return jax.shard_map(local, mesh=mesh, in_specs=in_specs, out_specs=out_specs, check_vma=False)
```

```python
import functools
import math

import jax
import jax.numpy as jnp
from jax import lax
from jax.experimental import pallas as pl
from jax.experimental.pallas import tpu as pltpu
from jax.sharding import PartitionSpec as P

axial_coupling = 0.5
SAMPLE_BLOCK = 8


def shifted(block, axes, sizes, delta):
    route = []
    for i in range(sizes[0]):
        for j in range(sizes[1]):
            si, sj = i - delta[0], j - delta[1]
            if 0 <= si < sizes[0] and 0 <= sj < sizes[1]:
                route.append((si * sizes[1] + sj, i * sizes[1] + j))
    return lax.ppermute(block, axes, route)


def fourier_rows(row_ids, sample_ids, sample_count):
    half_count = sample_count // 2
    harmonic = jnp.where(row_ids <= half_count, row_ids, row_ids - half_count)
    phase_index = harmonic[:, None] * sample_ids[None, :] % sample_count
    angle_value = phase_index.astype(jnp.float32) * (2.0 * math.pi / sample_count)
    dft_table = jnp.where(
        (row_ids <= half_count)[:, None], jnp.cos(angle_value), jnp.sin(angle_value)
    )
    return dft_table * math.sqrt(2.0 / sample_count)


def col_to_row(col, ix, iy):
    full = jnp.broadcast_to(col, ix.shape)
    return jnp.sum(jnp.where(ix == iy, full, 0.0), axis=0, keepdims=True)


def row_to_col(row, ix, iy):
    full = jnp.broadcast_to(row, ix.shape)
    return jnp.sum(jnp.where(ix == iy, full, 0.0), axis=1, keepdims=True)


def edges_kernel(a_ref, reg_ref, xlo_ref, xhi_ref, c127_ref, c0_ref, c1_ref, c2_ref):
    n_s, planes, nx, ny = a_ref.shape
    rows = planes * n_s
    ix = lax.broadcasted_iota(jnp.int32, (nx, ny), 0)
    iy = lax.broadcasted_iota(jnp.int32, (nx, ny), 1)
    regf = reg_ref[...].astype(jnp.float32)
    xlo_ref[pl.ds(rows, 8), :] = jnp.zeros((8, ny), jnp.float32)
    xlo_ref[pl.ds(rows, 1), :] = regf[nx - 1:nx, :]
    c127_ref[pl.ds(nx, 8), :] = jnp.zeros((8, ny), jnp.float32)
    c127_ref[pl.ds(nx, 1), :] = col_to_row(regf[:, ny - 1:ny], ix, iy)

    acc127 = jnp.zeros((nx, ny), jnp.float32)
    acc0 = jnp.zeros((nx, ny), jnp.float32)
    for s in range(n_s):
        for p in range(planes):
            t = s * planes + p
            a = a_ref[s, p]
            xlo_ref[pl.ds(p * n_s + s, 1), :] = a[nx - 1:nx, :]
            xhi_ref[pl.ds(p * n_s + s, 1), :] = a[0:1, :]
            acc127 = jnp.where(iy == t, pltpu.roll(a, (t + 1) % ny, 1), acc127)
            acc0 = jnp.where(iy == t, a if t == 0 else pltpu.roll(a, t, 1), acc0)
    c127_ref[pl.ds(0, nx), :] = acc127
    c0_ref[...] = acc0
    c1_ref[...] = acc0[nx - 1:nx, :]
    c2_ref[...] = acc127[0:1, :]


def edges(a, region):
    n_s, planes, nx, ny = a.shape
    rows = planes * n_s
    vmem = pl.BlockSpec(memory_space=pltpu.VMEM)
    f32 = jnp.float32
    shapes = [
        jax.ShapeDtypeStruct((rows + 8, ny), f32),
        jax.ShapeDtypeStruct((rows, ny), f32),
        jax.ShapeDtypeStruct((nx + 8, ny), f32),
        jax.ShapeDtypeStruct((nx, ny), f32),
        jax.ShapeDtypeStruct((1, ny), f32),
        jax.ShapeDtypeStruct((1, ny), f32),
    ]
    return pl.pallas_call(
        edges_kernel,
        in_specs=[vmem, vmem],
        out_specs=[vmem] * 6,
        out_shape=shapes,
        name="halo_edges",
    )(a, region)


def residual_kernel(kinds, levels, a_ref, src_ref, xlo_ref, xhi_ref, ylo_ref, yhi_ref, own0_ref, c2_ref,
                    c1_ref, level_ref, relu_ref, sat_ref, reg_ref, out_ref):
    blk = pl.program_id(0)
    n_s, planes, nx, ny = a_ref.shape
    n_all = n_s * pl.num_programs(0)
    rows = planes * n_all
    ix = lax.broadcasted_iota(jnp.int32, (nx, ny), 0)
    iy = lax.broadcasted_iota(jnp.int32, (nx, ny), 1)
    iy_row = lax.broadcasted_iota(jnp.int32, (1, ny), 1)
    reg = reg_ref[...]
    reg_xlo = xlo_ref[pl.ds(rows, 1), :].astype(jnp.int32)
    reg_ycol = row_to_col(ylo_ref[pl.ds(nx, 1), :], ix, iy).astype(jnp.int32)

    def lookup(kind, pick):
        out = jnp.broadcast_to(pick(0), kind.shape).astype(jnp.float32)
        for k in range(1, kinds):
            out = jnp.where(kind == k, pick(k), out)
        return out

    sat = lookup(reg, lambda k: sat_ref[k])
    sat_xlo = lookup(reg_xlo, lambda k: sat_ref[k])
    lane_sample = iy_row // planes
    lane_level = jnp.zeros((1, ny), jnp.int32)
    for s in range(n_all):
        lane_level = jnp.where(lane_sample == s, level_ref[s], lane_level)
    bt = []
    for k in range(kinds):
        row = jnp.full((1, ny), relu_ref[0, k], jnp.float32)
        for lv in range(1, levels):
            row = jnp.where(lane_level == lv, relu_ref[lv, k], row)
        bt.append(row)
    c_lo = ylo_ref[pl.ds(0, nx), :]
    lo_xp = jnp.where(ix == nx - 1, c2_ref[...], pltpu.roll(c_lo, nx - 1, 0))
    sx_c = lo_xp - c_lo
    sy_c = own0_ref[...] - c_lo
    kind_c = jnp.broadcast_to(reg_ycol, (nx, ny))
    base_c = lookup(kind_c, lambda k: bt[k])
    sat_c = lookup(kind_c, lambda k: sat_ref[k])
    fy_cols = base_c * (1.0 + sat_c * (sx_c * sx_c + sy_c * sy_c)) * sy_c
    c_hi = yhi_ref[...]

    def body(s, carry):
        s_glob = blk * n_s + s
        lv = level_ref[s_glob]
        base = lookup(reg, lambda k: relu_ref[lv, k])
        base_xlo = lookup(reg_xlo, lambda k: relu_ref[lv, k])
        tiles = [a_ref[s, p] for p in range(planes)]
        for p in range(planes):
            t = s_glob * planes + p
            a = tiles[p]
            row_hi = xhi_ref[pl.ds(p * n_all + s_glob, 1), :]
            row_lo = xlo_ref[pl.ds(p * n_all + s_glob, 1), :]
            c1 = c1_ref[0, t]
            col_hi = pltpu.roll(c_hi, lax.rem(ny - 1 - t + ny, ny), 1)
            a_xp = jnp.where(ix == nx - 1, row_hi, pltpu.roll(a, nx - 1, 0))
            a_yp = jnp.where(iy == ny - 1, col_hi, pltpu.roll(a, ny - 1, 1))
            sx = a_xp - a
            sy = a_yp - a
            rel = base * (1.0 + sat * (sx * sx + sy * sy))
            fx = rel * sx
            fy = rel * sy
            lo_yp = jnp.where(iy_row == ny - 1, c1, pltpu.roll(row_lo, ny - 1, 1))
            sx_l = a[0:1, :] - row_lo
            sy_l = lo_yp - row_lo
            fx_l = base_xlo * (1.0 + sat_xlo * (sx_l * sx_l + sy_l * sy_l)) * sx_l
            fy_c = pltpu.roll(fy_cols, lax.rem(ny - t, ny), 1)
            fx_down = jnp.where(ix == 0, fx_l, pltpu.roll(fx, 1, 0))
            fy_left = jnp.where(iy == 0, fy_c, pltpu.roll(fy, 1, 1))
            curl = fx_down - fx + fy_left - fy
            axial = 2.0 * a
            if p > 0:
                axial = axial - tiles[p - 1]
            if p < planes - 1:
                axial = axial - tiles[p + 1]
            out_ref[p, s] = curl + axial_coupling * axial - src_ref[s, p]
        return carry

    lax.fori_loop(0, n_s, body, 0)


def residual(a, src, xlo, xhi, ylo, yhi, own0, c2, c1, level_index, reluctivity, saturation, reg):
    n_s, planes, nx, ny = a.shape
    levels, kinds = reluctivity.shape
    sb = min(SAMPLE_BLOCK, n_s)
    tile = pl.BlockSpec((sb, planes, nx, ny), lambda i: (i, 0, 0, 0))
    vmem_whole = pl.BlockSpec(memory_space=pltpu.VMEM)
    smem_whole = pl.BlockSpec(memory_space=pltpu.SMEM)
    return pl.pallas_call(
        functools.partial(residual_kernel, kinds, levels),
        grid=(n_s // sb,),
        in_specs=[tile, tile] + [vmem_whole] * 6 + [smem_whole] * 4 + [vmem_whole],
        out_specs=pl.BlockSpec((planes, sb, nx, ny), lambda i: (0, i, 0, 0)),
        out_shape=jax.ShapeDtypeStruct((planes, n_s, nx, ny), jnp.float32),
        name="residual",
    )(a, src, xlo, xhi, ylo, yhi, own0, c2, c1, level_index, reluctivity, saturation, reg)


def local(potential, source, region, level_index, reluctivity, saturation, inverse, transmit):
    samples_dev, planes, cells_x, cells_y = potential.shape
    n_tm = lax.axis_size("tm")
    n_gx = lax.axis_size("gx")
    n_gy = lax.axis_size("gy")
    me_tm = lax.axis_index("tm")
    me_gx = lax.axis_index("gx")
    sample_count = samples_dev * n_tm
    q_dev = samples_dev
    grid = ("gx", "gy")
    sizes = (n_gx, n_gy)
    rows = planes * samples_dev

    gain_here = transmit[:, 0] * inverse[:, cells_x - 1, 0]
    own_info = jnp.concatenate([inverse[:, cells_x - 1, :], gain_here[:, None]], axis=1)
    infos = [own_info]
    for d in range(1, n_tm):
        infos.append(lax.ppermute(own_info, "tm", [(i, (i - d) % n_tm) for i in range(n_tm)]))
    info_all = jnp.concatenate(infos, axis=0)
    gain_all = info_all[:, cells_x]

    msg_xlo, msg_xhi, msg_c127, msg_c0, msg_c1, msg_c2 = edges(potential, region)
    xlo = shifted(msg_xlo, grid, sizes, (1, 0))
    xhi = shifted(msg_xhi, grid, sizes, (-1, 0))
    ylo = shifted(msg_c127, grid, sizes, (0, 1))
    yhi = shifted(msg_c0, grid, sizes, (0, -1))
    c1 = shifted(msg_c1, grid, sizes, (1, -1))
    c2 = shifted(msg_c2, grid, sizes, (-1, 1))
    resid = residual(potential, source, xlo, xhi, ylo, yhi, msg_c0, c2, c1, level_index, reluctivity,
                     saturation, region)

    sample_ids = me_tm * samples_dev + lax.iota(jnp.int32, samples_dev)
    tabs = [
        fourier_rows(((me_tm + d) % n_tm) * q_dev + lax.iota(jnp.int32, q_dev), sample_ids, sample_count)
        for d in range(n_tm)
    ]
    row_last = info_all[:, :cells_x].reshape(n_tm, q_dev, cells_x)
    parts = [jnp.einsum("qs,psxy->qpxy", tabs[d], resid, precision=lax.Precision.HIGH) for d in range(n_tm)]
    got_parts = [
        lax.ppermute(parts[d], "tm", [(i, (i + d) % n_tm) for i in range(n_tm)]) for d in range(1, n_tm)
    ]
    tails = jnp.concatenate(
        [jnp.einsum("qb,qpby->qpy", row_last[d], parts[d], precision=lax.Precision.HIGH) for d in range(n_tm)],
        axis=0,
    )
    msg_tail = jnp.concatenate([tails, jnp.broadcast_to(gain_all[:, None, None], (n_tm * q_dev, 1, cells_y))], axis=1)
    carried = jnp.zeros_like(tails)
    for d in range(n_gx - 1, 0, -1):
        got = lax.ppermute(msg_tail, "gx", [(i, i + d) for i in range(n_gx - d)])
        stepped = got[:, :planes] + got[:, planes:planes + 1] * carried
        carried = jnp.where(me_gx >= d, stepped, carried)
    carried = carried.reshape(n_tm, q_dev, planes, cells_y)
    got_carried = [
        lax.ppermute(carried[d], "tm", [(i, (i + d) % n_tm) for i in range(n_tm)]) for d in range(1, n_tm)
    ]
    spectrum = parts[0]
    for got in got_parts:
        spectrum = spectrum + got
    carried_own = carried[0]
    for got in got_carried:
        carried_own = carried_own + got
    solved = jnp.einsum("qab,qpby->qpay", inverse, spectrum, precision=lax.Precision.HIGH)
    injected = transmit[:, 0][:, None, None] * carried_own
    return solved + injected[:, :, None, :] * inverse[:, :, 0][:, None, :, None]


def solution(mesh):
    in_specs = (
        P("tm", None, "gx", "gy"),
        P("tm", None, "gx", "gy"),
        P("gx", "gy"),
        P("tm"),
        P(),
        P(),
        P("tm", "gx", None),
        P("tm", "gx"),
    )
    out_specs = P("tm", None, "gx", "gy")
    return jax.shard_map(local, mesh=mesh, in_specs=in_specs, out_specs=out_specs, check_vma=False)
```

```python
import functools
import math

import jax
import jax.numpy as jnp
from jax import lax
from jax.experimental import pallas as pl
from jax.experimental.pallas import tpu as pltpu
from jax.sharding import PartitionSpec as P

axial_coupling = 0.5
SAMPLE_BLOCK = 8


def shifted(block, axes, sizes, delta):
    route = []
    for i in range(sizes[0]):
        for j in range(sizes[1]):
            si, sj = i - delta[0], j - delta[1]
            if 0 <= si < sizes[0] and 0 <= sj < sizes[1]:
                route.append((si * sizes[1] + sj, i * sizes[1] + j))
    return lax.ppermute(block, axes, route)


def fourier_rows(row_ids, sample_ids, sample_count):
    half_count = sample_count // 2
    harmonic = jnp.where(row_ids <= half_count, row_ids, row_ids - half_count)
    phase_index = harmonic[:, None] * sample_ids[None, :] % sample_count
    angle_value = phase_index.astype(jnp.float32) * (2.0 * math.pi / sample_count)
    dft_table = jnp.where(
        (row_ids <= half_count)[:, None], jnp.cos(angle_value), jnp.sin(angle_value)
    )
    return dft_table * math.sqrt(2.0 / sample_count)


def col_to_row(col, ix, iy):
    full = jnp.broadcast_to(col, ix.shape)
    return jnp.sum(jnp.where(ix == iy, full, 0.0), axis=0, keepdims=True)


def row_to_col(row, ix, iy):
    full = jnp.broadcast_to(row, ix.shape)
    return jnp.sum(jnp.where(ix == iy, full, 0.0), axis=1, keepdims=True)


def edges_kernel(a_ref, reg_ref, xlo_ref, xhi_ref, c127_ref, c0_ref, c1_ref, c2_ref):
    n_s, planes, nx, ny = a_ref.shape
    rows = planes * n_s
    ix = lax.broadcasted_iota(jnp.int32, (nx, ny), 0)
    iy = lax.broadcasted_iota(jnp.int32, (nx, ny), 1)
    regf = reg_ref[...].astype(jnp.float32)
    xlo_ref[pl.ds(rows, 8), :] = jnp.zeros((8, ny), jnp.float32)
    xlo_ref[pl.ds(rows, 1), :] = regf[nx - 1:nx, :]
    c127_ref[pl.ds(nx, 8), :] = jnp.zeros((8, ny), jnp.float32)
    c127_ref[pl.ds(nx, 1), :] = col_to_row(regf[:, ny - 1:ny], ix, iy)

    acc127 = jnp.zeros((nx, ny), jnp.float32)
    acc0 = jnp.zeros((nx, ny), jnp.float32)
    for s in range(n_s):
        for p in range(planes):
            t = s * planes + p
            a = a_ref[s, p]
            xlo_ref[pl.ds(p * n_s + s, 1), :] = a[nx - 1:nx, :]
            xhi_ref[pl.ds(p * n_s + s, 1), :] = a[0:1, :]
            acc127 = jnp.where(iy == t, pltpu.roll(a, (t + 1) % ny, 1), acc127)
            acc0 = jnp.where(iy == t, a if t == 0 else pltpu.roll(a, t, 1), acc0)
    c127_ref[pl.ds(0, nx), :] = acc127
    c0_ref[...] = acc0
    c1_ref[...] = acc0[nx - 1:nx, :]
    c2_ref[...] = acc127[0:1, :]


def edges(a, region):
    n_s, planes, nx, ny = a.shape
    rows = planes * n_s
    vmem = pl.BlockSpec(memory_space=pltpu.VMEM)
    f32 = jnp.float32
    shapes = [
        jax.ShapeDtypeStruct((rows + 8, ny), f32),
        jax.ShapeDtypeStruct((rows, ny), f32),
        jax.ShapeDtypeStruct((nx + 8, ny), f32),
        jax.ShapeDtypeStruct((nx, ny), f32),
        jax.ShapeDtypeStruct((1, ny), f32),
        jax.ShapeDtypeStruct((1, ny), f32),
    ]
    return pl.pallas_call(
        edges_kernel,
        in_specs=[vmem, vmem],
        out_specs=[vmem] * 6,
        out_shape=shapes,
        name="halo_edges",
    )(a, region)


def residual_kernel(kinds, levels, a_ref, src_ref, xlo_ref, xhi_ref, ylo_ref, yhi_ref, own0_ref, c2_ref,
                    c1_ref, level_ref, relu_ref, sat_ref, reg_ref, out_ref):
    blk = pl.program_id(0)
    n_s, planes, nx, ny = a_ref.shape
    n_all = n_s * pl.num_programs(0)
    rows = planes * n_all
    ix = lax.broadcasted_iota(jnp.int32, (nx, ny), 0)
    iy = lax.broadcasted_iota(jnp.int32, (nx, ny), 1)
    iy_row = lax.broadcasted_iota(jnp.int32, (1, ny), 1)
    reg = reg_ref[...]
    reg_xlo = xlo_ref[pl.ds(rows, 1), :].astype(jnp.int32)
    reg_ycol = row_to_col(ylo_ref[pl.ds(nx, 1), :], ix, iy).astype(jnp.int32)

    def lookup(kind, pick):
        out = jnp.broadcast_to(pick(0), kind.shape).astype(jnp.float32)
        for k in range(1, kinds):
            out = jnp.where(kind == k, pick(k), out)
        return out

    sat = lookup(reg, lambda k: sat_ref[k])
    sat_xlo = lookup(reg_xlo, lambda k: sat_ref[k])
    lane_sample = iy_row // planes
    lane_level = jnp.zeros((1, ny), jnp.int32)
    for s in range(n_all):
        lane_level = jnp.where(lane_sample == s, level_ref[s], lane_level)
    bt = []
    for k in range(kinds):
        row = jnp.full((1, ny), relu_ref[0, k], jnp.float32)
        for lv in range(1, levels):
            row = jnp.where(lane_level == lv, relu_ref[lv, k], row)
        bt.append(row)
    c_lo = ylo_ref[pl.ds(0, nx), :]
    lo_xp = jnp.where(ix == nx - 1, c2_ref[...], pltpu.roll(c_lo, nx - 1, 0))
    sx_c = lo_xp - c_lo
    sy_c = own0_ref[...] - c_lo
    kind_c = jnp.broadcast_to(reg_ycol, (nx, ny))
    base_c = lookup(kind_c, lambda k: bt[k])
    sat_c = lookup(kind_c, lambda k: sat_ref[k])
    fy_cols = base_c * (1.0 + sat_c * (sx_c * sx_c + sy_c * sy_c)) * sy_c
    c_hi = yhi_ref[...]

    def body(s, carry):
        s_glob = blk * n_s + s
        lv = level_ref[s_glob]
        base = lookup(reg, lambda k: relu_ref[lv, k])
        base_xlo = lookup(reg_xlo, lambda k: relu_ref[lv, k])
        tiles = [a_ref[s, p] for p in range(planes)]
        for p in range(planes):
            t = s_glob * planes + p
            a = tiles[p]
            row_hi = xhi_ref[pl.ds(p * n_all + s_glob, 1), :]
            row_lo = xlo_ref[pl.ds(p * n_all + s_glob, 1), :]
            c1 = c1_ref[0, t]
            col_hi = pltpu.roll(c_hi, lax.rem(ny - 1 - t + ny, ny), 1)
            a_xp = jnp.where(ix == nx - 1, row_hi, pltpu.roll(a, nx - 1, 0))
            a_yp = jnp.where(iy == ny - 1, col_hi, pltpu.roll(a, ny - 1, 1))
            sx = a_xp - a
            sy = a_yp - a
            rel = base * (1.0 + sat * (sx * sx + sy * sy))
            fx = rel * sx
            fy = rel * sy
            lo_yp = jnp.where(iy_row == ny - 1, c1, pltpu.roll(row_lo, ny - 1, 1))
            sx_l = a[0:1, :] - row_lo
            sy_l = lo_yp - row_lo
            fx_l = base_xlo * (1.0 + sat_xlo * (sx_l * sx_l + sy_l * sy_l)) * sx_l
            fy_c = pltpu.roll(fy_cols, lax.rem(ny - t, ny), 1)
            fx_down = jnp.where(ix == 0, fx_l, pltpu.roll(fx, 1, 0))
            fy_left = jnp.where(iy == 0, fy_c, pltpu.roll(fy, 1, 1))
            curl = fx_down - fx + fy_left - fy
            axial = 2.0 * a
            if p > 0:
                axial = axial - tiles[p - 1]
            if p < planes - 1:
                axial = axial - tiles[p + 1]
            out_ref[p, s] = curl + axial_coupling * axial - src_ref[s, p]
        return carry

    lax.fori_loop(0, n_s, body, 0)


def residual(a, src, xlo, xhi, ylo, yhi, own0, c2, c1, level_index, reluctivity, saturation, reg):
    n_s, planes, nx, ny = a.shape
    levels, kinds = reluctivity.shape
    sb = min(SAMPLE_BLOCK, n_s)
    tile = pl.BlockSpec((sb, planes, nx, ny), lambda i: (i, 0, 0, 0))
    vmem_whole = pl.BlockSpec(memory_space=pltpu.VMEM)
    smem_whole = pl.BlockSpec(memory_space=pltpu.SMEM)
    return pl.pallas_call(
        functools.partial(residual_kernel, kinds, levels),
        grid=(n_s // sb,),
        in_specs=[tile, tile] + [vmem_whole] * 6 + [smem_whole] * 4 + [vmem_whole],
        out_specs=pl.BlockSpec((planes, sb, nx, ny), lambda i: (0, i, 0, 0)),
        out_shape=jax.ShapeDtypeStruct((planes, n_s, nx, ny), jnp.float32),
        name="residual",
    )(a, src, xlo, xhi, ylo, yhi, own0, c2, c1, level_index, reluctivity, saturation, reg)


def post_kernel(own_ref, recv_ref, inv_ref, inj_ref, out_ref):
    n_q, planes = own_ref.shape[:2]
    for q in range(n_q):
        m = inv_ref[q]
        col0 = m[:, 0:1]
        for p in range(planes):
            spectrum = own_ref[q, p] + recv_ref[q, p]
            solved = jnp.dot(m, spectrum, precision=lax.Precision.HIGHEST, preferred_element_type=jnp.float32)
            out_ref[q, p] = solved + inj_ref[q, pl.ds(p, 1), :] * col0


def post(own, recv, inverse, inj):
    n_q, planes, nx, ny = own.shape
    qb = 4 if n_q % 4 == 0 else 1
    tile = pl.BlockSpec((qb, planes, nx, ny), lambda i: (i, 0, 0, 0))
    return pl.pallas_call(
        post_kernel,
        grid=(n_q // qb,),
        in_specs=[tile, tile, pl.BlockSpec((qb, nx, nx), lambda i: (i, 0, 0)),
                  pl.BlockSpec((qb, planes, ny), lambda i: (i, 0, 0))],
        out_specs=tile,
        out_shape=jax.ShapeDtypeStruct(own.shape, jnp.float32),
        name="block_solve",
    )(own, recv, inverse, inj)


def local(potential, source, region, level_index, reluctivity, saturation, inverse, transmit):
    samples_dev, planes, cells_x, cells_y = potential.shape
    n_tm = lax.axis_size("tm")
    n_gx = lax.axis_size("gx")
    n_gy = lax.axis_size("gy")
    me_tm = lax.axis_index("tm")
    me_gx = lax.axis_index("gx")
    sample_count = samples_dev * n_tm
    q_dev = samples_dev
    grid = ("gx", "gy")
    sizes = (n_gx, n_gy)
    rows = planes * samples_dev

    gain_here = transmit[:, 0] * inverse[:, cells_x - 1, 0]
    own_info = jnp.concatenate([inverse[:, cells_x - 1, :], gain_here[:, None]], axis=1)
    infos = [own_info]
    for d in range(1, n_tm):
        infos.append(lax.ppermute(own_info, "tm", [(i, (i - d) % n_tm) for i in range(n_tm)]))
    info_all = jnp.concatenate(infos, axis=0)
    gain_all = info_all[:, cells_x]

    msg_xlo, msg_xhi, msg_c127, msg_c0, msg_c1, msg_c2 = edges(potential, region)
    xlo = shifted(msg_xlo, grid, sizes, (1, 0))
    xhi = shifted(msg_xhi, grid, sizes, (-1, 0))
    ylo = shifted(msg_c127, grid, sizes, (0, 1))
    yhi = shifted(msg_c0, grid, sizes, (0, -1))
    c1 = shifted(msg_c1, grid, sizes, (1, -1))
    c2 = shifted(msg_c2, grid, sizes, (-1, 1))
    resid = residual(potential, source, xlo, xhi, ylo, yhi, msg_c0, c2, c1, level_index, reluctivity,
                     saturation, region)

    sample_ids = me_tm * samples_dev + lax.iota(jnp.int32, samples_dev)
    tabs = [
        fourier_rows(((me_tm + d) % n_tm) * q_dev + lax.iota(jnp.int32, q_dev), sample_ids, sample_count)
        for d in range(n_tm)
    ]
    row_last = info_all[:, :cells_x].reshape(n_tm, q_dev, cells_x)
    parts = [jnp.einsum("qs,psxy->qpxy", tabs[d], resid, precision=lax.Precision.HIGH) for d in range(n_tm)]
    got_parts = [
        lax.ppermute(parts[d], "tm", [(i, (i + d) % n_tm) for i in range(n_tm)]) for d in range(1, n_tm)
    ]
    tails = jnp.concatenate(
        [jnp.einsum("qb,qpby->qpy", row_last[d], parts[d], precision=lax.Precision.HIGH) for d in range(n_tm)],
        axis=0,
    )
    msg_tail = jnp.concatenate([tails, jnp.broadcast_to(gain_all[:, None, None], (n_tm * q_dev, 1, cells_y))], axis=1)
    carried = jnp.zeros_like(tails)
    for d in range(n_gx - 1, 0, -1):
        got = lax.ppermute(msg_tail, "gx", [(i, i + d) for i in range(n_gx - d)])
        stepped = got[:, :planes] + got[:, planes:planes + 1] * carried
        carried = jnp.where(me_gx >= d, stepped, carried)
    carried = carried.reshape(n_tm, q_dev, planes, cells_y)
    got_carried = [
        lax.ppermute(carried[d], "tm", [(i, (i + d) % n_tm) for i in range(n_tm)]) for d in range(1, n_tm)
    ]
    recv = got_parts[0]
    for got in got_parts[1:]:
        recv = recv + got
    carried_own = carried[0]
    for got in got_carried:
        carried_own = carried_own + got
    injected = transmit[:, 0][:, None, None] * carried_own
    return post(parts[0], recv, inverse, injected)


def solution(mesh):
    in_specs = (
        P("tm", None, "gx", "gy"),
        P("tm", None, "gx", "gy"),
        P("gx", "gy"),
        P("tm"),
        P(),
        P(),
        P("tm", "gx", None),
        P("tm", "gx"),
    )
    out_specs = P("tm", None, "gx", "gy")
    return jax.shard_map(local, mesh=mesh, in_specs=in_specs, out_specs=out_specs, check_vma=False)
```

```python
import functools
import math

import jax
import jax.numpy as jnp
from jax import lax
from jax.experimental import pallas as pl
from jax.experimental.pallas import tpu as pltpu
from jax.sharding import PartitionSpec as P

axial_coupling = 0.5
SAMPLE_BLOCK = 8


def shifted(block, axes, sizes, delta):
    route = []
    for i in range(sizes[0]):
        for j in range(sizes[1]):
            si, sj = i - delta[0], j - delta[1]
            if 0 <= si < sizes[0] and 0 <= sj < sizes[1]:
                route.append((si * sizes[1] + sj, i * sizes[1] + j))
    return lax.ppermute(block, axes, route)


def fourier_rows(row_ids, sample_ids, sample_count):
    half_count = sample_count // 2
    harmonic = jnp.where(row_ids <= half_count, row_ids, row_ids - half_count)
    phase_index = harmonic[:, None] * sample_ids[None, :] % sample_count
    angle_value = phase_index.astype(jnp.float32) * (2.0 * math.pi / sample_count)
    dft_table = jnp.where(
        (row_ids <= half_count)[:, None], jnp.cos(angle_value), jnp.sin(angle_value)
    )
    return dft_table * math.sqrt(2.0 / sample_count)


def col_to_row(col, ix, iy):
    full = jnp.broadcast_to(col, ix.shape)
    return jnp.sum(jnp.where(ix == iy, full, 0.0), axis=0, keepdims=True)


def row_to_col(row, ix, iy):
    full = jnp.broadcast_to(row, ix.shape)
    return jnp.sum(jnp.where(ix == iy, full, 0.0), axis=1, keepdims=True)


def edges_kernel(a_ref, reg_ref, xlo_ref, xhi_ref, c127_ref, c0_ref):
    n_s, planes, nx, ny = a_ref.shape
    rows = planes * n_s
    ix = lax.broadcasted_iota(jnp.int32, (nx, ny), 0)
    iy = lax.broadcasted_iota(jnp.int32, (nx, ny), 1)
    regf = reg_ref[...].astype(jnp.float32)
    xlo_ref[pl.ds(rows, 8), :] = jnp.zeros((8, ny), jnp.float32)
    xlo_ref[pl.ds(rows, 1), :] = regf[nx - 1:nx, :]
    xhi_ref[pl.ds(rows, 8), :] = jnp.zeros((8, ny), jnp.float32)
    c127_ref[pl.ds(nx, 8), :] = jnp.zeros((8, ny), jnp.float32)
    c127_ref[pl.ds(nx, 1), :] = col_to_row(regf[:, ny - 1:ny], ix, iy)

    acc127 = jnp.zeros((nx, ny), jnp.float32)
    acc0 = jnp.zeros((nx, ny), jnp.float32)
    for s in range(n_s):
        for p in range(planes):
            t = s * planes + p
            a = a_ref[s, p]
            xlo_ref[pl.ds(p * n_s + s, 1), :] = a[nx - 1:nx, :]
            xhi_ref[pl.ds(p * n_s + s, 1), :] = a[0:1, :]
            acc127 = jnp.where(iy == t, pltpu.roll(a, (t + 1) % ny, 1), acc127)
            acc0 = jnp.where(iy == t, a if t == 0 else pltpu.roll(a, t, 1), acc0)
    c127_ref[pl.ds(0, nx), :] = acc127
    c0_ref[...] = acc0


def edges(a, region):
    n_s, planes, nx, ny = a.shape
    rows = planes * n_s
    vmem = pl.BlockSpec(memory_space=pltpu.VMEM)
    f32 = jnp.float32
    shapes = [
        jax.ShapeDtypeStruct((rows + 8, ny), f32),
        jax.ShapeDtypeStruct((rows + 8, ny), f32),
        jax.ShapeDtypeStruct((nx + 8, ny), f32),
        jax.ShapeDtypeStruct((nx, ny), f32),
    ]
    return pl.pallas_call(
        edges_kernel,
        in_specs=[vmem, vmem],
        out_specs=[vmem] * 4,
        out_shape=shapes,
        name="halo_edges",
    )(a, region)


def residual_kernel(kinds, levels, a_ref, src_ref, xlo_ref, xhi_ref, ylo_ref, yhi_ref, own0_ref,
                    level_ref, relu_ref, sat_ref, reg_ref, out_ref):
    blk = pl.program_id(0)
    n_s, planes, nx, ny = a_ref.shape
    n_all = n_s * pl.num_programs(0)
    rows = planes * n_all
    ix = lax.broadcasted_iota(jnp.int32, (nx, ny), 0)
    iy = lax.broadcasted_iota(jnp.int32, (nx, ny), 1)
    iy_row = lax.broadcasted_iota(jnp.int32, (1, ny), 1)
    reg = reg_ref[...]
    reg_xlo = xlo_ref[pl.ds(rows, 1), :].astype(jnp.int32)
    reg_ycol = row_to_col(ylo_ref[pl.ds(nx, 1), :], ix, iy).astype(jnp.int32)

    def lookup(kind, pick):
        out = jnp.broadcast_to(pick(0), kind.shape).astype(jnp.float32)
        for k in range(1, kinds):
            out = jnp.where(kind == k, pick(k), out)
        return out

    sat = lookup(reg, lambda k: sat_ref[k])
    sat_xlo = lookup(reg_xlo, lambda k: sat_ref[k])
    lane_sample = iy_row // planes
    lane_level = jnp.zeros((1, ny), jnp.int32)
    for s in range(n_all):
        lane_level = jnp.where(lane_sample == s, level_ref[s], lane_level)
    bt = []
    for k in range(kinds):
        row = jnp.full((1, ny), relu_ref[0, k], jnp.float32)
        for lv in range(1, levels):
            row = jnp.where(lane_level == lv, relu_ref[lv, k], row)
        bt.append(row)
    c_lo = ylo_ref[pl.ds(0, nx), :]
    lo_xp = jnp.where(ix == nx - 1, xhi_ref[pl.ds(rows, 1), :], pltpu.roll(c_lo, nx - 1, 0))
    c1_row = xlo_ref[pl.ds(rows + 1, 1), :]
    sx_c = lo_xp - c_lo
    sy_c = own0_ref[...] - c_lo
    kind_c = jnp.broadcast_to(reg_ycol, (nx, ny))
    base_c = lookup(kind_c, lambda k: bt[k])
    sat_c = lookup(kind_c, lambda k: sat_ref[k])
    fy_cols = base_c * (1.0 + sat_c * (sx_c * sx_c + sy_c * sy_c)) * sy_c
    c_hi = yhi_ref[...]

    def body(s, carry):
        s_glob = blk * n_s + s
        lv = level_ref[s_glob]
        base = lookup(reg, lambda k: relu_ref[lv, k])
        base_xlo = lookup(reg_xlo, lambda k: relu_ref[lv, k])
        tiles = [a_ref[s, p] for p in range(planes)]
        for p in range(planes):
            t = s_glob * planes + p
            a = tiles[p]
            row_hi = xhi_ref[pl.ds(p * n_all + s_glob, 1), :]
            row_lo = xlo_ref[pl.ds(p * n_all + s_glob, 1), :]
            c1 = pltpu.roll(c1_row, lax.rem(ny - 1 - t + ny, ny), 1)
            col_hi = pltpu.roll(c_hi, lax.rem(ny - 1 - t + ny, ny), 1)
            a_xp = jnp.where(ix == nx - 1, row_hi, pltpu.roll(a, nx - 1, 0))
            a_yp = jnp.where(iy == ny - 1, col_hi, pltpu.roll(a, ny - 1, 1))
            sx = a_xp - a
            sy = a_yp - a
            rel = base * (1.0 + sat * (sx * sx + sy * sy))
            fx = rel * sx
            fy = rel * sy
            lo_yp = jnp.where(iy_row == ny - 1, c1, pltpu.roll(row_lo, ny - 1, 1))
            sx_l = a[0:1, :] - row_lo
            sy_l = lo_yp - row_lo
            fx_l = base_xlo * (1.0 + sat_xlo * (sx_l * sx_l + sy_l * sy_l)) * sx_l
            fy_c = pltpu.roll(fy_cols, lax.rem(ny - t, ny), 1)
            fx_down = jnp.where(ix == 0, fx_l, pltpu.roll(fx, 1, 0))
            fy_left = jnp.where(iy == 0, fy_c, pltpu.roll(fy, 1, 1))
            curl = fx_down - fx + fy_left - fy
            axial = 2.0 * a
            if p > 0:
                axial = axial - tiles[p - 1]
            if p < planes - 1:
                axial = axial - tiles[p + 1]
            out_ref[p, s] = curl + axial_coupling * axial - src_ref[s, p]
        return carry

    lax.fori_loop(0, n_s, body, 0)


def residual(a, src, xlo, xhi, ylo, yhi, own0, level_index, reluctivity, saturation, reg):
    n_s, planes, nx, ny = a.shape
    levels, kinds = reluctivity.shape
    sb = min(SAMPLE_BLOCK, n_s)
    tile = pl.BlockSpec((sb, planes, nx, ny), lambda i: (i, 0, 0, 0))
    vmem_whole = pl.BlockSpec(memory_space=pltpu.VMEM)
    smem_whole = pl.BlockSpec(memory_space=pltpu.SMEM)
    return pl.pallas_call(
        functools.partial(residual_kernel, kinds, levels),
        grid=(n_s // sb,),
        in_specs=[tile, tile] + [vmem_whole] * 5 + [smem_whole] * 3 + [vmem_whole],
        out_specs=pl.BlockSpec((planes, sb, nx, ny), lambda i: (0, i, 0, 0)),
        out_shape=jax.ShapeDtypeStruct((planes, n_s, nx, ny), jnp.float32),
        name="residual",
    )(a, src, xlo, xhi, ylo, yhi, own0, level_index, reluctivity, saturation, reg)


def local(potential, source, region, level_index, reluctivity, saturation, inverse, transmit):
    samples_dev, planes, cells_x, cells_y = potential.shape
    n_tm = lax.axis_size("tm")
    n_gx = lax.axis_size("gx")
    n_gy = lax.axis_size("gy")
    me_tm = lax.axis_index("tm")
    me_gx = lax.axis_index("gx")
    sample_count = samples_dev * n_tm
    q_dev = samples_dev
    grid = ("gx", "gy")
    sizes = (n_gx, n_gy)
    rows = planes * samples_dev

    gain_here = transmit[:, 0] * inverse[:, cells_x - 1, 0]
    own_info = jnp.concatenate([inverse[:, cells_x - 1, :], gain_here[:, None]], axis=1)
    infos = [own_info]
    for d in range(1, n_tm):
        infos.append(lax.ppermute(own_info, "tm", [(i, (i - d) % n_tm) for i in range(n_tm)]))
    info_all = jnp.concatenate(infos, axis=0)
    gain_all = info_all[:, cells_x]

    msg_xlo, msg_xhi, msg_c127, msg_c0 = edges(potential, region)
    ylo = shifted(msg_c127, grid, sizes, (0, 1))
    yhi = shifted(msg_c0, grid, sizes, (0, -1))
    msg_xlo = lax.dynamic_update_slice_in_dim(msg_xlo, yhi[cells_x - 1:cells_x], rows + 1, 0)
    msg_xhi = lax.dynamic_update_slice_in_dim(msg_xhi, ylo[0:1], rows, 0)
    xlo = shifted(msg_xlo, grid, sizes, (1, 0))
    xhi = shifted(msg_xhi, grid, sizes, (-1, 0))
    resid = residual(potential, source, xlo, xhi, ylo, yhi, msg_c0, level_index, reluctivity,
                     saturation, region)

    sample_ids = me_tm * samples_dev + lax.iota(jnp.int32, samples_dev)
    tabs = [
        fourier_rows(((me_tm + d) % n_tm) * q_dev + lax.iota(jnp.int32, q_dev), sample_ids, sample_count)
        for d in range(n_tm)
    ]
    row_last = info_all[:, :cells_x].reshape(n_tm, q_dev, cells_x)
    parts = [jnp.einsum("qs,psxy->qpxy", tabs[d], resid, precision=lax.Precision.HIGH) for d in range(n_tm)]
    got_parts = [
        lax.ppermute(parts[d], "tm", [(i, (i + d) % n_tm) for i in range(n_tm)]) for d in range(1, n_tm)
    ]
    tails = jnp.concatenate(
        [jnp.einsum("qb,qpby->qpy", row_last[d], parts[d], precision=lax.Precision.HIGH) for d in range(n_tm)],
        axis=0,
    )
    msg_tail = jnp.concatenate([tails, jnp.broadcast_to(gain_all[:, None, None], (n_tm * q_dev, 1, cells_y))], axis=1)
    carried = jnp.zeros_like(tails)
    for d in range(n_gx - 1, 0, -1):
        got = lax.ppermute(msg_tail, "gx", [(i, i + d) for i in range(n_gx - d)])
        stepped = got[:, :planes] + got[:, planes:planes + 1] * carried
        carried = jnp.where(me_gx >= d, stepped, carried)
    carried = carried.reshape(n_tm, q_dev, planes, cells_y)
    got_carried = [
        lax.ppermute(carried[d], "tm", [(i, (i + d) % n_tm) for i in range(n_tm)]) for d in range(1, n_tm)
    ]
    spectrum = parts[0]
    for got in got_parts:
        spectrum = spectrum + got
    carried_own = carried[0]
    for got in got_carried:
        carried_own = carried_own + got
    solved = jnp.einsum("qab,qpby->qpay", inverse, spectrum, precision=lax.Precision.HIGH)
    injected = transmit[:, 0][:, None, None] * carried_own
    return solved + injected[:, :, None, :] * inverse[:, :, 0][:, None, :, None]


def solution(mesh):
    in_specs = (
        P("tm", None, "gx", "gy"),
        P("tm", None, "gx", "gy"),
        P("gx", "gy"),
        P("tm"),
        P(),
        P(),
        P("tm", "gx", None),
        P("tm", "gx"),
    )
    out_specs = P("tm", None, "gx", "gy")
    return jax.shard_map(local, mesh=mesh, in_specs=in_specs, out_specs=out_specs, check_vma=False)
```

```python
import functools
import math

import jax
import jax.numpy as jnp
from jax import lax
from jax.experimental import pallas as pl
from jax.experimental.pallas import tpu as pltpu
from jax.sharding import PartitionSpec as P

axial_coupling = 0.5
SAMPLE_BLOCK = 8


def shifted(block, axes, sizes, delta):
    route = []
    for i in range(sizes[0]):
        for j in range(sizes[1]):
            si, sj = i - delta[0], j - delta[1]
            if 0 <= si < sizes[0] and 0 <= sj < sizes[1]:
                route.append((si * sizes[1] + sj, i * sizes[1] + j))
    return lax.ppermute(block, axes, route)


def fourier_rows(row_ids, sample_ids, sample_count):
    half_count = sample_count // 2
    harmonic = jnp.where(row_ids <= half_count, row_ids, row_ids - half_count)
    phase_index = harmonic[:, None] * sample_ids[None, :] % sample_count
    angle_value = phase_index.astype(jnp.float32) * (2.0 * math.pi / sample_count)
    dft_table = jnp.where(
        (row_ids <= half_count)[:, None], jnp.cos(angle_value), jnp.sin(angle_value)
    )
    return dft_table * math.sqrt(2.0 / sample_count)


def col_to_row(col, ix, iy):
    full = jnp.broadcast_to(col, ix.shape)
    return jnp.sum(jnp.where(ix == iy, full, 0.0), axis=0, keepdims=True)


def row_to_col(row, ix, iy):
    full = jnp.broadcast_to(row, ix.shape)
    return jnp.sum(jnp.where(ix == iy, full, 0.0), axis=1, keepdims=True)


def edges_kernel(a_ref, reg_ref, xlo_ref, xhi_ref, c127_ref, c0_ref, c1_ref, c2_ref):
    n_s, planes, nx, ny = a_ref.shape
    rows = planes * n_s
    ix = lax.broadcasted_iota(jnp.int32, (nx, ny), 0)
    iy = lax.broadcasted_iota(jnp.int32, (nx, ny), 1)
    regf = reg_ref[...].astype(jnp.float32)
    xlo_ref[pl.ds(rows, 8), :] = jnp.zeros((8, ny), jnp.float32)
    xlo_ref[pl.ds(rows, 1), :] = regf[nx - 1:nx, :]
    c127_ref[pl.ds(nx, 8), :] = jnp.zeros((8, ny), jnp.float32)
    c127_ref[pl.ds(nx, 1), :] = col_to_row(regf[:, ny - 1:ny], ix, iy)

    acc127 = jnp.zeros((nx, ny), jnp.float32)
    acc0 = jnp.zeros((nx, ny), jnp.float32)
    for s in range(n_s):
        for p in range(planes):
            t = s * planes + p
            a = a_ref[s, p]
            xlo_ref[pl.ds(p * n_s + s, 1), :] = a[nx - 1:nx, :]
            xhi_ref[pl.ds(p * n_s + s, 1), :] = a[0:1, :]
            acc127 = jnp.where(iy == t, pltpu.roll(a, (t + 1) % ny, 1), acc127)
            acc0 = jnp.where(iy == t, a if t == 0 else pltpu.roll(a, t, 1), acc0)
    c127_ref[pl.ds(0, nx), :] = acc127
    c0_ref[...] = acc0
    c1_ref[...] = acc0[nx - 1:nx, :]
    c2_ref[...] = acc127[0:1, :]


def edges(a, region):
    n_s, planes, nx, ny = a.shape
    rows = planes * n_s
    vmem = pl.BlockSpec(memory_space=pltpu.VMEM)
    f32 = jnp.float32
    shapes = [
        jax.ShapeDtypeStruct((rows + 8, ny), f32),
        jax.ShapeDtypeStruct((rows, ny), f32),
        jax.ShapeDtypeStruct((nx + 8, ny), f32),
        jax.ShapeDtypeStruct((nx, ny), f32),
        jax.ShapeDtypeStruct((1, ny), f32),
        jax.ShapeDtypeStruct((1, ny), f32),
    ]
    return pl.pallas_call(
        edges_kernel,
        in_specs=[vmem, vmem],
        out_specs=[vmem] * 6,
        out_shape=shapes,
        name="halo_edges",
    )(a, region)


def residual_kernel(kinds, levels, a_ref, src_ref, xlo_ref, xhi_ref, ylo_ref, yhi_ref, own0_ref, c2_ref,
                    c1_ref, level_ref, relu_ref, sat_ref, reg_ref, out_ref):
    blk = pl.program_id(0)
    n_s, planes, nx, ny = a_ref.shape
    n_all = n_s * pl.num_programs(0)
    rows = planes * n_all
    ix = lax.broadcasted_iota(jnp.int32, (nx, ny), 0)
    iy = lax.broadcasted_iota(jnp.int32, (nx, ny), 1)
    iy_row = lax.broadcasted_iota(jnp.int32, (1, ny), 1)
    reg = reg_ref[...]
    reg_xlo = xlo_ref[pl.ds(rows, 1), :].astype(jnp.int32)
    reg_ycol = row_to_col(ylo_ref[pl.ds(nx, 1), :], ix, iy).astype(jnp.int32)

    def lookup(kind, pick):
        out = jnp.broadcast_to(pick(0), kind.shape).astype(jnp.float32)
        for k in range(1, kinds):
            out = jnp.where(kind == k, pick(k), out)
        return out

    sat = lookup(reg, lambda k: sat_ref[k])
    sat_xlo = lookup(reg_xlo, lambda k: sat_ref[k])
    lane_sample = iy_row // planes
    lane_level = jnp.zeros((1, ny), jnp.int32)
    for s in range(n_all):
        lane_level = jnp.where(lane_sample == s, level_ref[s], lane_level)
    bt = []
    for k in range(kinds):
        row = jnp.full((1, ny), relu_ref[0, k], jnp.float32)
        for lv in range(1, levels):
            row = jnp.where(lane_level == lv, relu_ref[lv, k], row)
        bt.append(row)
    c_lo = ylo_ref[pl.ds(0, nx), :]
    lo_xp = jnp.where(ix == nx - 1, c2_ref[...], pltpu.roll(c_lo, nx - 1, 0))
    sx_c = lo_xp - c_lo
    sy_c = own0_ref[...] - c_lo
    kind_c = jnp.broadcast_to(reg_ycol, (nx, ny))
    base_c = lookup(kind_c, lambda k: bt[k])
    sat_c = lookup(kind_c, lambda k: sat_ref[k])
    fy_cols = base_c * (1.0 + sat_c * (sx_c * sx_c + sy_c * sy_c)) * sy_c
    c_hi = yhi_ref[...]

    def body(s, carry):
        s_glob = blk * n_s + s
        lv = level_ref[s_glob]
        base = lookup(reg, lambda k: relu_ref[lv, k])
        base_xlo = lookup(reg_xlo, lambda k: relu_ref[lv, k])
        tiles = [a_ref[s, p] for p in range(planes)]
        for p in range(planes):
            t = s_glob * planes + p
            a = tiles[p]
            row_hi = xhi_ref[pl.ds(p * n_all + s_glob, 1), :]
            row_lo = xlo_ref[pl.ds(p * n_all + s_glob, 1), :]
            c1 = c1_ref[0, t]
            col_hi = pltpu.roll(c_hi, lax.rem(ny - 1 - t + ny, ny), 1)
            a_xp = jnp.where(ix == nx - 1, row_hi, pltpu.roll(a, nx - 1, 0))
            a_yp = jnp.where(iy == ny - 1, col_hi, pltpu.roll(a, ny - 1, 1))
            sx = a_xp - a
            sy = a_yp - a
            rel = base * (1.0 + sat * (sx * sx + sy * sy))
            fx = rel * sx
            fy = rel * sy
            lo_yp = jnp.where(iy_row == ny - 1, c1, pltpu.roll(row_lo, ny - 1, 1))
            sx_l = a[0:1, :] - row_lo
            sy_l = lo_yp - row_lo
            fx_l = base_xlo * (1.0 + sat_xlo * (sx_l * sx_l + sy_l * sy_l)) * sx_l
            fy_c = pltpu.roll(fy_cols, lax.rem(ny - t, ny), 1)
            fx_down = jnp.where(ix == 0, fx_l, pltpu.roll(fx, 1, 0))
            fy_left = jnp.where(iy == 0, fy_c, pltpu.roll(fy, 1, 1))
            curl = fx_down - fx + fy_left - fy
            axial = 2.0 * a
            if p > 0:
                axial = axial - tiles[p - 1]
            if p < planes - 1:
                axial = axial - tiles[p + 1]
            out_ref[p, s] = curl + axial_coupling * axial - src_ref[s, p]
        return carry

    lax.fori_loop(0, n_s, body, 0, unroll=2)


def residual(a, src, xlo, xhi, ylo, yhi, own0, c2, c1, level_index, reluctivity, saturation, reg):
    n_s, planes, nx, ny = a.shape
    levels, kinds = reluctivity.shape
    sb = min(SAMPLE_BLOCK, n_s)
    tile = pl.BlockSpec((sb, planes, nx, ny), lambda i: (i, 0, 0, 0))
    vmem_whole = pl.BlockSpec(memory_space=pltpu.VMEM)
    smem_whole = pl.BlockSpec(memory_space=pltpu.SMEM)
    return pl.pallas_call(
        functools.partial(residual_kernel, kinds, levels),
        grid=(n_s // sb,),
        in_specs=[tile, tile] + [vmem_whole] * 6 + [smem_whole] * 4 + [vmem_whole],
        out_specs=pl.BlockSpec((planes, sb, nx, ny), lambda i: (0, i, 0, 0)),
        out_shape=jax.ShapeDtypeStruct((planes, n_s, nx, ny), jnp.float32),
        name="residual",
    )(a, src, xlo, xhi, ylo, yhi, own0, c2, c1, level_index, reluctivity, saturation, reg)


def local(potential, source, region, level_index, reluctivity, saturation, inverse, transmit):
    samples_dev, planes, cells_x, cells_y = potential.shape
    n_tm = lax.axis_size("tm")
    n_gx = lax.axis_size("gx")
    n_gy = lax.axis_size("gy")
    me_tm = lax.axis_index("tm")
    me_gx = lax.axis_index("gx")
    sample_count = samples_dev * n_tm
    q_dev = samples_dev
    grid = ("gx", "gy")
    sizes = (n_gx, n_gy)
    rows = planes * samples_dev

    gain_here = transmit[:, 0] * inverse[:, cells_x - 1, 0]
    own_info = jnp.concatenate([inverse[:, cells_x - 1, :], gain_here[:, None]], axis=1)
    infos = [own_info]
    for d in range(1, n_tm):
        infos.append(lax.ppermute(own_info, "tm", [(i, (i - d) % n_tm) for i in range(n_tm)]))
    info_all = jnp.concatenate(infos, axis=0)
    gain_all = info_all[:, cells_x]

    msg_xlo, msg_xhi, msg_c127, msg_c0, msg_c1, msg_c2 = edges(potential, region)
    xlo = shifted(msg_xlo, grid, sizes, (1, 0))
    xhi = shifted(msg_xhi, grid, sizes, (-1, 0))
    ylo = shifted(msg_c127, grid, sizes, (0, 1))
    yhi = shifted(msg_c0, grid, sizes, (0, -1))
    c1 = shifted(msg_c1, grid, sizes, (1, -1))
    c2 = shifted(msg_c2, grid, sizes, (-1, 1))
    resid = residual(potential, source, xlo, xhi, ylo, yhi, msg_c0, c2, c1, level_index, reluctivity,
                     saturation, region)

    sample_ids = me_tm * samples_dev + lax.iota(jnp.int32, samples_dev)
    tabs = [
        fourier_rows(((me_tm + d) % n_tm) * q_dev + lax.iota(jnp.int32, q_dev), sample_ids, sample_count)
        for d in range(n_tm)
    ]
    row_last = info_all[:, :cells_x].reshape(n_tm, q_dev, cells_x)
    parts = [jnp.einsum("qs,psxy->qpxy", tabs[d], resid, precision=lax.Precision.HIGH) for d in range(n_tm)]
    got_parts = [
        lax.ppermute(parts[d], "tm", [(i, (i + d) % n_tm) for i in range(n_tm)]) for d in range(1, n_tm)
    ]
    tails = jnp.concatenate(
        [jnp.einsum("qb,qpby->qpy", row_last[d], parts[d], precision=lax.Precision.HIGH) for d in range(n_tm)],
        axis=0,
    )
    msg_tail = jnp.concatenate([tails, jnp.broadcast_to(gain_all[:, None, None], (n_tm * q_dev, 1, cells_y))], axis=1)
    carried = jnp.zeros_like(tails)
    for d in range(n_gx - 1, 0, -1):
        got = lax.ppermute(msg_tail, "gx", [(i, i + d) for i in range(n_gx - d)])
        stepped = got[:, :planes] + got[:, planes:planes + 1] * carried
        carried = jnp.where(me_gx >= d, stepped, carried)
    carried = carried.reshape(n_tm, q_dev, planes, cells_y)
    got_carried = [
        lax.ppermute(carried[d], "tm", [(i, (i + d) % n_tm) for i in range(n_tm)]) for d in range(1, n_tm)
    ]
    spectrum = parts[0]
    for got in got_parts:
        spectrum = spectrum + got
    carried_own = carried[0]
    for got in got_carried:
        carried_own = carried_own + got
    solved = jnp.einsum("qab,qpby->qpay", inverse, spectrum, precision=lax.Precision.HIGH)
    injected = transmit[:, 0][:, None, None] * carried_own
    return solved + injected[:, :, None, :] * inverse[:, :, 0][:, None, :, None]


def solution(mesh):
    in_specs = (
        P("tm", None, "gx", "gy"),
        P("tm", None, "gx", "gy"),
        P("gx", "gy"),
        P("tm"),
        P(),
        P(),
        P("tm", "gx", None),
        P("tm", "gx"),
    )
    out_specs = P("tm", None, "gx", "gy")
    return jax.shard_map(local, mesh=mesh, in_specs=in_specs, out_specs=out_specs, check_vma=False)
```
